512 devices in a mesh: exc: 8 (over y_lo, core), line: 64 (over z, x, y_hi).
Axes of the slice: x: 4, y: 8 (y_hi: 2, y_lo: 4; y = y_hi * 4 + y_lo), z: 8, core: 2. Of those that a mesh axis runs over, the one named last changes fastest.
Arguments:
- adj_e: float32 [3, 8, 1024, 1024], P(None, 'exc', 'line'), parts along dimension 1, may hold values from -6 to 6
- adj_h: float32 [3, 8, 1024, 1024], P(None, 'exc', 'line'), parts along dimension 1, may hold values from -6 to 6
- fwd_e: bfloat16 [2, 3, 8, 1024, 1024], P(None, None, 'exc', 'line'), parts along dimension 2, may hold values from -6 to 6
- permittivity: float32 [1, 1024, 1024], P(None, 'line'), may hold values from 1 to 6
- design_mask: int32 [1, 1024, 1024], P(None, 'line'), may hold values 0 or 1
- inverse: bfloat16 [1024, 1024], replicated, may hold values from -0.03125 to 0.6875
- omega: float32 [8], P('exc'), parts along dimension 0, may hold values from 0.3 to 2.5
- port_mode: float32 [8192], P('exc'), parts along dimension 0, may hold values from -6 to 6
- port_plane: int32 [8], P('exc'), parts along dimension 0, may hold values from 0 to 1023
Outputs:
- adj_e_out: float32 [3, 8, 1024, 1024], P(None, 'exc', 'line'), parts along dimension 1
- adj_h_out: float32 [3, 8, 1024, 1024], P(None, 'exc', 'line'), parts along dimension 1
- gradient: float32 [8, 1024, 1024], P('exc', 'line'), parts along dimension 0
The draws below stay inside these ranges and needn't reach their ends.
There are 8 independent parts, one for each index of `exc`. The reference program is written for one: setup_inputs(seed, part) draws one part's arguments, and reference() takes and returns one part's arrays. A program takes and returns all parts, laid end to end along the dimension named above; an argument that names none is the same for every part. Nothing has to cross between parts.
All inputs are finite; a program needn't handle non-finite values. No bound on the sum of `design_mask` on one device may be relied on, other than what follows from the above.
Results may differ from the reference program's by a relative error of at most 0.005.
Values may be sent and summed in bfloat16 or wider, within the bound.
No kernel may reach another device: no remote copies, remote signals or barrier semaphores. Data moves between devices by JAX's collectives and lax.ppermute only.
A program may use at most 64 MiB of HBM per device.

```python
import math
import jax
import jax.numpy as jnp
from jax import lax

CELLS = 1024
PLANES = 1
STEPS = 2


def draw_inverse(key, part):
    diag_key, off_key = jax.random.split(key)
    diagonal = jax.random.uniform(diag_key, (CELLS,), jnp.float32, 0.5, 0.6875)
    spread = jax.random.uniform(off_key, (CELLS, CELLS), jnp.float32, -0.03125, 0.03125)
    identity = jnp.arange(CELLS)[:, None] == jnp.arange(CELLS)[None, :]
    return jnp.where(identity, diagonal[None, :], spread).astype(jnp.bfloat16)


def set_ends(drawn, key, least, top_value):
    extent = drawn.shape
    place = [jax.random.randint(jax.random.fold_in(key, axis), (), 0, extent[axis]) for axis in range(len(extent))]
    drawn = drawn.at[tuple(place)].set(least)
    longest = extent.index(max(extent))
    place[longest] = (place[longest] + 1) % extent[longest]
    return drawn.at[tuple(place)].set(top_value)


def block_scale(rng, extent, shards, least, largest):
    level, own = 1.0, jax.random.fold_in(rng, 6)
    for dim, blocks in shards:
        heights = jnp.exp(jax.random.uniform(jax.random.fold_in(own, dim), (blocks,), jnp.float32, least / len(shards), largest / len(shards)))
        level = level * jnp.repeat(heights, extent[dim] // blocks).reshape([-1 if axis == dim else 1 for axis in range(len(extent))])
    return level


def normal_values(own_key, dims, width, bound, cuts=(), kind=jnp.bfloat16):
    entries = jax.random.normal(own_key, dims, jnp.float32) * width
    if len(cuts) > 0:
        entries = block_scale(own_key, dims, cuts, -0.22, 0.18) * entries
    return jnp.clip(entries, min=-bound, max=bound).astype(kind)


def setup_inputs(seed: int = 0, part: int = 0) -> dict:
    arg_keys = jax.random.split(jax.random.key(seed), 10)
    part_splits = jax.random.split(jax.random.fold_in(arg_keys[9], part), 10)
    return {
        "adj_e": normal_values(part_splits[0], (3, PLANES, CELLS, CELLS), 1.0, 6.0, ((2, 64),), jnp.float32),
        "adj_h": normal_values(part_splits[1], (3, PLANES, CELLS, CELLS), 1.0, 6.0, ((2, 64),), jnp.float32),
        "fwd_e": normal_values(part_splits[2], (STEPS, 3, PLANES, CELLS, CELLS), 1.0, 6.0, ((3, 64),)),
        "permittivity": jnp.clip(jnp.exp(math.log(6.0) - 1.7917595 * jax.random.uniform(arg_keys[3], (PLANES, CELLS, CELLS), jnp.float32) ** block_scale(arg_keys[3], (PLANES, CELLS, CELLS), ((1, 64),), -0.2, 0.2)), 1.0, 6.0),
        "design_mask": set_ends((jax.random.randint(arg_keys[4], (PLANES, CELLS, CELLS), 0, 2) < 1).astype(jnp.int32), jax.random.fold_in(arg_keys[4], 1), 0, 1),
        "inverse": draw_inverse(jax.random.fold_in(arg_keys[9], 71), part),
        "omega": jnp.clip(jnp.exp(jax.random.uniform(part_splits[6], (1,), jnp.float32, math.log(0.3), math.log(2.5))), 0.3, 2.5),
        "port_mode": normal_values(part_splits[7], (CELLS,), 1.0, 6.0, (), jnp.float32),
        "port_plane": jax.random.randint(part_splits[8], (1,), 0, CELLS).astype(jnp.int32),
    }


COURANT = 0.4


def lower_diff(padded, along):
    inner = padded.shape[along] - 2
    middle = lax.slice_in_dim(padded, 1, inner + 1, axis=along)
    return middle - lax.slice_in_dim(padded, 0, inner, axis=along)


def upper_diff(padded, along):
    inner = padded.shape[along] - 2
    middle = lax.slice_in_dim(padded, 1, inner + 1, axis=along)
    return lax.slice_in_dim(padded, 2, inner + 2, axis=along) - middle


def zero_rim(stacked, along):
    widths = [(0, 0)] * stacked.ndim
    widths[along] = (1, 1)
    return jnp.pad(stacked, widths)


def curl_along_y(fields, inverse_eps, extend, along):
    electric_x, electric_y, electric_z = fields[0], fields[1], fields[2]
    magnetic_x, magnetic_y, magnetic_z = fields[3], fields[4], fields[5]
    scaled = COURANT * inverse_eps
    lower_terms = lower_diff(extend(jnp.stack([magnetic_x, magnetic_z]), along), along)
    electric_x = electric_x + scaled * lower_terms[1]
    electric_z = electric_z - scaled * lower_terms[0]
    upper_terms = upper_diff(extend(jnp.stack([electric_x, electric_z]), along), along)
    magnetic_x = magnetic_x - COURANT * upper_terms[1]
    magnetic_z = magnetic_z + COURANT * upper_terms[0]
    return jnp.stack([electric_x, electric_y, electric_z, magnetic_x, magnetic_y, magnetic_z])


def curl_along_xz(fields, inverse_eps, extend, along):
    electric_x, electric_y, electric_z = fields[0], fields[1], fields[2]
    magnetic_x, magnetic_y, magnetic_z = fields[3], fields[4], fields[5]
    scaled = COURANT * inverse_eps
    depth_terms = lower_diff(zero_rim(jnp.stack([magnetic_x, magnetic_y]), 1), 1)
    across = lower_diff(extend(jnp.stack([magnetic_y, magnetic_z]), along), along)
    electric_x = electric_x - scaled * depth_terms[1]
    electric_y = electric_y + scaled * (depth_terms[0] - across[1])
    electric_z = electric_z + scaled * across[0]
    depth_upper = upper_diff(zero_rim(jnp.stack([electric_x, electric_y]), 1), 1)
    across_upper = upper_diff(extend(jnp.stack([electric_y, electric_z]), along), along)
    magnetic_x = magnetic_x + COURANT * depth_upper[1]
    magnetic_y = magnetic_y + COURANT * (across_upper[1] - depth_upper[0])
    magnetic_z = magnetic_z - COURANT * across_upper[0]
    return jnp.stack([electric_x, electric_y, electric_z, magnetic_x, magnetic_y, magnetic_z])


def line_solve(rounded, inverse):
    flattened = rounded.reshape(-1, rounded.shape[-1])
    solved = lax.dot_general(flattened, inverse, (((1,), (1,)), ((), ())), preferred_element_type=jnp.float32)
    return solved.reshape(rounded.shape)


def reference(adj_e, adj_h, fwd_e, permittivity, design_mask, inverse, omega, port_mode, port_plane):
    fields = jnp.concatenate([adj_e, adj_h], 0)
    inverse_rows = 1.0 / permittivity
    inverse_cols = jnp.swapaxes(inverse_rows, 1, 2)
    frequency = omega[0]
    profile = port_mode
    column = (jnp.arange(CELLS, dtype=jnp.int32) == port_plane[0]).astype(jnp.float32)
    mask_weight = design_mask.astype(jnp.float32)
    gradient = jnp.zeros((PLANES, CELLS, CELLS), jnp.float32)
    for instant in range(STEPS):
        amplitude = jnp.cos(frequency * (instant + 1))
        fields = fields.at[2].add((amplitude * profile[None, :, None]) * column[None, None, :])
        fields = curl_along_y(fields, inverse_rows, zero_rim, 2)
        fields = line_solve(fields.astype(jnp.bfloat16), inverse)
        fields = curl_along_xz(fields, inverse_rows, zero_rim, 3)
        turned = jnp.swapaxes(fields.astype(jnp.bfloat16), 2, 3)
        fields = line_solve(turned, inverse)
        snapshot = fwd_e[instant].astype(jnp.float32)
        intersection = fields[0] * snapshot[0] + fields[1] * snapshot[1] + fields[2] * snapshot[2]
        gradient = gradient + mask_weight * intersection * (inverse_cols * inverse_cols)
        if instant + 1 < STEPS:
            fields = jnp.swapaxes(fields, 2, 3)
    return fields[:3], fields[3:], gradient
```

```python
import jax
import jax.numpy as jnp
from jax import lax
from jax.sharding import PartitionSpec as P

COURANT = 0.4


def line_solve(rounded, inverse):
    flattened = rounded.reshape(-1, rounded.shape[-1])
    solved = lax.dot_general(
        flattened, inverse, (((1,), (1,)), ((), ())), preferred_element_type=jnp.float32
    )
    return solved.reshape(rounded.shape)


def turn(block, line_count):
    strip = block.shape[-2]
    lead = block.shape[:-2]
    n = len(lead)
    parts = block.reshape(lead + (strip, line_count, strip))
    parts = jnp.moveaxis(parts, n + 1, 0)
    parts = lax.all_to_all(parts, "line", 0, 0, tiled=True)
    order = tuple(range(1, n + 1)) + (n + 2, 0, n + 1)
    parts = jnp.transpose(parts, order)
    return parts.reshape(lead + (strip, line_count * strip))


def shift_down(f, along, first):
    inner = f.shape[along]
    return jnp.concatenate([first, lax.slice_in_dim(f, 0, inner - 1, axis=along)], axis=along)


def shift_up(f, along, last):
    inner = f.shape[along]
    return jnp.concatenate([lax.slice_in_dim(f, 1, inner, axis=along), last], axis=along)


def zeros_like_slice(f, along):
    shape = list(f.shape)
    shape[along] = 1
    return jnp.zeros(shape, f.dtype)


def curl_y(fields, scaled, along, below=None, above=None):
    ex, ey, ez, hx, hy, hz = fields
    if below is None:
        below = (zeros_like_slice(hx, along), zeros_like_slice(hz, along))
    if above is None:
        z = zeros_like_slice(hx, along)
        above = (z, z, z, z, z)
    hx_prev = shift_down(hx, along, below[0])
    hz_prev = shift_down(hz, along, below[1])
    ex = ex + scaled * (hz - hz_prev)
    ez = ez - scaled * (hx - hx_prev)
    last = lax.slice_in_dim(hx, hx.shape[along] - 1, hx.shape[along], axis=along)
    last_z = lax.slice_in_dim(hz, hz.shape[along] - 1, hz.shape[along], axis=along)
    ex_a, ez_a, hx_a, hz_a, scaled_a = above
    ex_next_edge = ex_a + scaled_a * (hz_a - last_z)
    ez_next_edge = ez_a - scaled_a * (hx_a - last)
    ex_next = shift_up(ex, along, ex_next_edge)
    ez_next = shift_up(ez, along, ez_next_edge)
    hx = hx - COURANT * (ez_next - ez)
    hz = hz + COURANT * (ex_next - ex)
    return (ex, ey, ez, hx, hy, hz)


def curl_xz(fields, scaled, along_x, along_z):
    ex, ey, ez, hx, hy, hz = fields

    def lower(f, along):
        return f - shift_down(f, along, zeros_like_slice(f, along))

    def upper(f, along):
        return shift_up(f, along, zeros_like_slice(f, along)) - f

    ex = ex - scaled * lower(hy, along_z)
    ey = ey + scaled * (lower(hx, along_z) - lower(hz, along_x))
    ez = ez + scaled * lower(hy, along_x)
    hx = hx + COURANT * upper(ey, along_z)
    hy = hy + COURANT * (upper(ez, along_x) - upper(ex, along_z))
    hz = hz - COURANT * upper(ey, along_x)
    return (ex, ey, ez, hx, hy, hz)


def per_device(
    adj_e, adj_h, fwd_e, permittivity, design_mask, inverse, omega, port_mode, port_plane
):
    line_cells = inverse.shape[0]
    strip = adj_e.shape[2]
    step_count = fwd_e.shape[0]
    line_count = lax.axis_size("line")
    index = lax.axis_index("line")
    offset = index * strip
    inverse_rows = 1.0 / permittivity
    inverse_cols = turn(inverse_rows, line_count)
    scaled_rows = COURANT * inverse_rows
    scaled_cols = COURANT * inverse_cols
    frequency = omega[0]
    plane_at = port_plane[0]
    mask_weight = design_mask.astype(jnp.float32)
    gradient = jnp.zeros(design_mask.shape, jnp.float32)

    fields = tuple(adj_e[i] for i in range(3)) + tuple(adj_h[i] for i in range(3))
    column = (jnp.arange(line_cells, dtype=jnp.int32) == plane_at).astype(jnp.float32)
    profile_rows = lax.dynamic_slice_in_dim(port_mode, offset, strip)
    amplitude = jnp.cos(frequency * 1.0)
    ex, ey, ez, hx, hy, hz = fields
    ez = ez + (amplitude * profile_rows[None, :, None]) * column[None, None, :]
    fields = (ex, ey, ez, hx, hy, hz)
    rows_along = 1
    up = [(i, i + 1) for i in range(line_count - 1)]
    down = [(i + 1, i) for i in range(line_count - 1)]
    last_rows = jnp.stack([hx[:, -1:], hz[:, -1:]])
    first_rows = jnp.stack(
        [ex[:, :1], ez[:, :1], hx[:, :1], hz[:, :1], scaled_rows[:, :1]]
    )
    below = lax.ppermute(last_rows, "line", up)
    above = lax.ppermute(first_rows, "line", down)
    fields = curl_y(
        fields,
        scaled_rows,
        rows_along,
        below=(below[0], below[1]),
        above=tuple(above[i] for i in range(5)),
    )
    for instant in range(step_count):
        if instant > 0:
            amplitude = jnp.cos(frequency * (instant + 1))
            x_local = offset + jnp.arange(strip, dtype=jnp.int32)
            column_local = (x_local == plane_at).astype(jnp.float32)
            ex, ey, ez, hx, hy, hz = fields
            ez = ez + (amplitude * column_local[None, :, None]) * port_mode[None, None, :]
            fields = curl_y((ex, ey, ez, hx, hy, hz), scaled_cols, 2)
            rounded = jnp.stack(fields).astype(jnp.bfloat16)
            rounded = turn(rounded, line_count)
        else:
            rounded = jnp.stack(fields).astype(jnp.bfloat16)
        solved = line_solve(rounded, inverse)
        fields = tuple(solved[i] for i in range(6))
        fields = curl_xz(fields, scaled_rows, 2, 0)
        rounded = jnp.stack(fields).astype(jnp.bfloat16)
        rounded = turn(rounded, line_count)
        solved = line_solve(rounded, inverse)
        fields = tuple(solved[i] for i in range(6))
        snapshot = fwd_e[instant].astype(jnp.float32)
        intersection = fields[0] * snapshot[0] + fields[1] * snapshot[1] + fields[2] * snapshot[2]
        gradient = gradient + mask_weight * intersection * (inverse_cols * inverse_cols)
    out = jnp.stack(fields)
    return (out[:3], out[3:], gradient)


def solution(mesh):
    in_specs = (
        P(None, "exc", "line", None),
        P(None, "exc", "line", None),
        P(None, None, "exc", "line", None),
        P(None, "line", None),
        P(None, "line", None),
        P(),
        P("exc"),
        P("exc"),
        P("exc"),
    )
    out_specs = (P(None, "exc", "line", None), P(None, "exc", "line", None), P("exc", "line", None))
    return jax.shard_map(
        per_device, mesh=mesh, in_specs=in_specs, out_specs=out_specs, check_vma=False
    )
```

```python
import jax
import jax.numpy as jnp
from jax import lax
from jax.sharding import PartitionSpec as P

COURANT = 0.4


def line_solve(rounded, inverse):
    flattened = rounded.reshape(-1, rounded.shape[-1])
    solved = lax.dot_general(
        flattened, inverse, (((1,), (1,)), ((), ())), preferred_element_type=jnp.float32
    )
    return solved.reshape(rounded.shape)


def turn_rows(block, line_count):
    comps, strip, cells = block.shape
    parts = block.reshape(comps, strip, line_count, strip)
    parts = jnp.transpose(parts, (2, 1, 0, 3)).reshape(line_count, strip, comps * strip)
    parts = lax.all_to_all(parts, "line", 0, 0, tiled=True)
    return parts.reshape(line_count * strip, comps * strip)


def solve_turned(turned, inverse):
    return lax.dot_general(
        turned, inverse, (((0,), (1,)), ((), ())), preferred_element_type=jnp.float32
    )


def bf16_parts(values):
    high = lax.reduce_precision(values, exponent_bits=8, mantissa_bits=7)
    rest = values - high
    middle = lax.reduce_precision(rest, exponent_bits=8, mantissa_bits=7)
    return [high, middle, rest - middle]


def shift_down(f, along, first):
    inner = f.shape[along]
    return jnp.concatenate([first, lax.slice_in_dim(f, 0, inner - 1, axis=along)], axis=along)


def shift_up(f, along, last):
    inner = f.shape[along]
    return jnp.concatenate([lax.slice_in_dim(f, 1, inner, axis=along), last], axis=along)


def zeros_like_slice(f, along):
    shape = list(f.shape)
    shape[along] = 1
    return jnp.zeros(shape, f.dtype)


def curl_y(fields, scaled, along, below=None, above=None):
    ex, ey, ez, hx, hy, hz = fields
    if below is None:
        below = (zeros_like_slice(hx, along), zeros_like_slice(hz, along))
    if above is None:
        z = zeros_like_slice(hx, along)
        above = (z, z, z, z, z)
    hx_prev = shift_down(hx, along, below[0])
    hz_prev = shift_down(hz, along, below[1])
    ex = ex + scaled * (hz - hz_prev)
    ez = ez - scaled * (hx - hx_prev)
    last = lax.slice_in_dim(hx, hx.shape[along] - 1, hx.shape[along], axis=along)
    last_z = lax.slice_in_dim(hz, hz.shape[along] - 1, hz.shape[along], axis=along)
    ex_a, ez_a, hx_a, hz_a, scaled_a = above
    ex_next_edge = ex_a + scaled_a * (hz_a - last_z)
    ez_next_edge = ez_a - scaled_a * (hx_a - last)
    ex_next = shift_up(ex, along, ex_next_edge)
    ez_next = shift_up(ez, along, ez_next_edge)
    hx = hx - COURANT * (ez_next - ez)
    hz = hz + COURANT * (ex_next - ex)
    return (ex, ey, ez, hx, hy, hz)


def curl_xz(fields, scaled, along_x, along_z):
    ex, ey, ez, hx, hy, hz = fields

    def lower(f, along):
        return f - shift_down(f, along, zeros_like_slice(f, along))

    def upper(f, along):
        return shift_up(f, along, zeros_like_slice(f, along)) - f

    ex = ex - scaled * lower(hy, along_z)
    ey = ey + scaled * (lower(hx, along_z) - lower(hz, along_x))
    ez = ez + scaled * lower(hy, along_x)
    hx = hx + COURANT * upper(ey, along_z)
    hy = hy + COURANT * (upper(ez, along_x) - upper(ex, along_z))
    hz = hz - COURANT * upper(ey, along_x)
    return (ex, ey, ez, hx, hy, hz)


def per_device(
    adj_e, adj_h, fwd_e, permittivity, design_mask, inverse, omega, port_mode, port_plane
):
    line_cells = inverse.shape[0]
    strip = adj_e.shape[2]
    planes = adj_e.shape[1]
    eps_planes = permittivity.shape[0]
    step_count = fwd_e.shape[0]
    line_count = lax.axis_size("line")
    index = lax.axis_index("line")
    offset = index * strip
    inverse_rows = 1.0 / permittivity
    scaled_rows = COURANT * inverse_rows
    frequency = omega[0]
    plane_at = port_plane[0]
    mask_weight = design_mask.astype(jnp.float32)
    gradient = jnp.zeros(design_mask.shape, jnp.float32)
    comps = 6 * planes

    column = (jnp.arange(line_cells, dtype=jnp.int32) == plane_at).astype(jnp.float32)
    profile_rows = lax.dynamic_slice_in_dim(port_mode, offset, strip)
    amplitude = jnp.cos(frequency * 1.0)
    ex, ey, ez = adj_e[0], adj_e[1], adj_e[2]
    hx, hy, hz = adj_h[0], adj_h[1], adj_h[2]
    ez = ez + (amplitude * profile_rows[None, :, None]) * column[None, None, :]
    up = [(i, i + 1) for i in range(line_count - 1)]
    down = [(i + 1, i) for i in range(line_count - 1)]
    last_rows = jnp.stack([hx[:, -1:], hz[:, -1:]])
    first_rows = jnp.stack(
        [ex[:, :1], ez[:, :1], hx[:, :1], hz[:, :1], jnp.broadcast_to(scaled_rows[:, :1], ex[:, :1].shape)]
    )
    below = lax.ppermute(last_rows, "line", up)
    above = lax.ppermute(first_rows, "line", down)
    fields = curl_y(
        (ex, ey, ez, hx, hy, hz),
        scaled_rows,
        1,
        below=(below[0], below[1]),
        above=tuple(above[i] for i in range(5)),
    )
    inverse_cols = None
    for instant in range(step_count):
        if instant > 0:
            amplitude = jnp.cos(frequency * (instant + 1))
            x_local = offset + jnp.arange(strip, dtype=jnp.int32)
            column_local = (x_local == plane_at).astype(jnp.float32)
            ex, ey, ez, hx, hy, hz = fields
            ez = ez + (amplitude * column_local[None, :, None]) * port_mode[None, None, :]
            fields = curl_y((ex, ey, ez, hx, hy, hz), COURANT * inverse_cols, 2)
            rounded = jnp.stack(fields).reshape(comps, strip, line_cells).astype(jnp.bfloat16)
            solved = solve_turned(turn_rows(rounded, line_count), inverse)
        else:
            rounded = jnp.stack(fields).astype(jnp.bfloat16)
            solved = line_solve(rounded, inverse)
        solved = solved.reshape(6, planes, strip, line_cells)
        fields = curl_xz(tuple(solved[i] for i in range(6)), scaled_rows, 2, 0)
        stacked = jnp.stack(fields).reshape(comps, strip, line_cells)
        if inverse_cols is None:
            stacked = jnp.concatenate([stacked] + bf16_parts(inverse_rows), 0)
        turned = turn_rows(stacked.astype(jnp.bfloat16), line_count)
        if inverse_cols is None:
            width = eps_planes * strip
            pieces = [
                turned[:, comps * strip + k * width : comps * strip + (k + 1) * width].astype(jnp.float32)
                for k in range(3)
            ]
            joined = (pieces[0] + pieces[1]) + pieces[2]
            inverse_cols = joined.T.reshape(eps_planes, strip, line_cells)
            turned = turned[:, : comps * strip]
        solved = solve_turned(turned, inverse).reshape(6, planes, strip, line_cells)
        fields = tuple(solved[i] for i in range(6))
        snapshot = fwd_e[instant].astype(jnp.float32)
        intersection = fields[0] * snapshot[0] + fields[1] * snapshot[1] + fields[2] * snapshot[2]
        gradient = gradient + mask_weight * intersection * (inverse_cols * inverse_cols)
    out = jnp.stack(fields)
    return (out[:3], out[3:], gradient)


def solution(mesh):
    in_specs = (
        P(None, "exc", "line", None),
        P(None, "exc", "line", None),
        P(None, None, "exc", "line", None),
        P(None, "line", None),
        P(None, "line", None),
        P(),
        P("exc"),
        P("exc"),
        P("exc"),
    )
    out_specs = (P(None, "exc", "line", None), P(None, "exc", "line", None), P("exc", "line", None))
    return jax.shard_map(
        per_device, mesh=mesh, in_specs=in_specs, out_specs=out_specs, check_vma=False
    )
```

```python
import jax
import jax.numpy as jnp
from jax import lax
from jax.sharding import PartitionSpec as P

COURANT = 0.4


def line_solve(rounded, inverse):
    flattened = rounded.reshape(-1, rounded.shape[-1])
    solved = lax.dot_general(
        flattened, inverse, (((1,), (1,)), ((), ())), preferred_element_type=jnp.float32
    )
    return solved.reshape(rounded.shape)


def turn_rows(block, line_count):
    comps, strip, cells = block.shape
    parts = block.reshape(comps, strip, line_count, strip)
    parts = jnp.transpose(parts, (2, 1, 0, 3)).reshape(line_count, strip, comps * strip)
    parts = lax.all_to_all(parts, "line", 0, 0, tiled=True)
    return parts.reshape(line_count * strip, comps * strip)


def solve_turned(turned, inverse):
    return lax.dot_general(
        turned, inverse, (((0,), (1,)), ((), ())), preferred_element_type=jnp.float32
    )


def bf16_parts(values):
    high = lax.reduce_precision(values, exponent_bits=8, mantissa_bits=7)
    return [high, values - high]


def shift_down(f, along, first):
    inner = f.shape[along]
    return jnp.concatenate([first, lax.slice_in_dim(f, 0, inner - 1, axis=along)], axis=along)


def shift_up(f, along, last):
    inner = f.shape[along]
    return jnp.concatenate([lax.slice_in_dim(f, 1, inner, axis=along), last], axis=along)


def zeros_like_slice(f, along):
    shape = list(f.shape)
    shape[along] = 1
    return jnp.zeros(shape, f.dtype)


def curl_y(fields, scaled, along, below=None, above=None):
    ex, ey, ez, hx, hy, hz = fields
    if below is None:
        below = (zeros_like_slice(hx, along), zeros_like_slice(hz, along))
    if above is None:
        z = zeros_like_slice(hx, along)
        above = (z, z, z, z, z)
    hx_prev = shift_down(hx, along, below[0])
    hz_prev = shift_down(hz, along, below[1])
    ex = ex + scaled * (hz - hz_prev)
    ez = ez - scaled * (hx - hx_prev)
    last = lax.slice_in_dim(hx, hx.shape[along] - 1, hx.shape[along], axis=along)
    last_z = lax.slice_in_dim(hz, hz.shape[along] - 1, hz.shape[along], axis=along)
    ex_a, ez_a, hx_a, hz_a, scaled_a = above
    ex_next_edge = ex_a + scaled_a * (hz_a - last_z)
    ez_next_edge = ez_a - scaled_a * (hx_a - last)
    ex_next = shift_up(ex, along, ex_next_edge)
    ez_next = shift_up(ez, along, ez_next_edge)
    hx = hx - COURANT * (ez_next - ez)
    hz = hz + COURANT * (ex_next - ex)
    return (ex, ey, ez, hx, hy, hz)


def curl_xz(fields, scaled, along_x, along_z):
    ex, ey, ez, hx, hy, hz = fields

    def lower(f, along):
        return f - shift_down(f, along, zeros_like_slice(f, along))

    def upper(f, along):
        return shift_up(f, along, zeros_like_slice(f, along)) - f

    ex = ex - scaled * lower(hy, along_z)
    ey = ey + scaled * (lower(hx, along_z) - lower(hz, along_x))
    ez = ez + scaled * lower(hy, along_x)
    hx = hx + COURANT * upper(ey, along_z)
    hy = hy + COURANT * (upper(ez, along_x) - upper(ex, along_z))
    hz = hz - COURANT * upper(ey, along_x)
    return (ex, ey, ez, hx, hy, hz)


def per_device(
    adj_e, adj_h, fwd_e, permittivity, design_mask, inverse, omega, port_mode, port_plane
):
    line_cells = inverse.shape[0]
    strip = adj_e.shape[2]
    planes = adj_e.shape[1]
    eps_planes = permittivity.shape[0]
    step_count = fwd_e.shape[0]
    line_count = lax.axis_size("line")
    index = lax.axis_index("line")
    offset = index * strip
    inverse_rows = 1.0 / permittivity
    scaled_rows = COURANT * inverse_rows
    frequency = omega[0]
    plane_at = port_plane[0]
    mask_weight = design_mask.astype(jnp.float32)
    gradient = jnp.zeros(design_mask.shape, jnp.float32)
    comps = 6 * planes

    column = (jnp.arange(line_cells, dtype=jnp.int32) == plane_at).astype(jnp.float32)
    profile_rows = lax.dynamic_slice_in_dim(port_mode, offset, strip)
    amplitude = jnp.cos(frequency * 1.0)
    ex, ey, ez = adj_e[0], adj_e[1], adj_e[2]
    hx, hy, hz = adj_h[0], adj_h[1], adj_h[2]
    ez = ez + (amplitude * profile_rows[None, :, None]) * column[None, None, :]
    is_first = index == 0
    ring = [(i, (i + 1) % line_count) for i in range(line_count)]
    scaled_planes = jnp.broadcast_to(scaled_rows, ex.shape)
    message = jnp.stack(
        [f[:, -1:] for f in (ex, ey, ez, hx, hy, hz, scaled_planes)] + [hx[:, -2:-1], hz[:, -2:-1]]
    )
    message = lax.ppermute(message, "line", ring)
    p_ex, p_ey, p_ez, p_hx, p_hy, p_hz, p_r, p_hx2, p_hz2 = (message[i] for i in range(9))
    zero_row = jnp.zeros_like(p_hx)
    hx_prev = shift_down(hx, 1, jnp.where(is_first, zero_row, p_hx))
    hz_prev = shift_down(hz, 1, jnp.where(is_first, zero_row, p_hz))
    ex1 = ex + scaled_rows * (hz - hz_prev)
    ez1 = ez - scaled_rows * (hx - hx_prev)
    hx1 = hx[:, :-1] - COURANT * (ez1[:, 1:] - ez1[:, :-1])
    hz1 = hz[:, :-1] + COURANT * (ex1[:, 1:] - ex1[:, :-1])
    ex_y = p_ex + p_r * (p_hz - p_hz2)
    ez_y = p_ez - p_r * (p_hx - p_hx2)
    ex_next = jnp.where(is_first, zero_row, ex1[:, :1])
    ez_next = jnp.where(is_first, zero_row, ez1[:, :1])
    hx_y = p_hx - COURANT * (ez_next - ez_y)
    hz_y = p_hz + COURANT * (ex_next - ex_y)
    fields = (
        jnp.concatenate([ex_y, ex1[:, :-1]], 1),
        jnp.concatenate([p_ey, ey[:, :-1]], 1),
        jnp.concatenate([ez_y, ez1[:, :-1]], 1),
        jnp.concatenate([hx_y, hx1], 1),
        jnp.concatenate([p_hy, hy[:, :-1]], 1),
        jnp.concatenate([hz_y, hz1], 1),
    )
    scaled_held = jnp.concatenate([p_r[:eps_planes], scaled_rows[:, :-1]], 1)
    inverse_held = jnp.roll(inverse, 1, axis=1)
    inverse_cols = None
    for instant in range(step_count):
        if instant > 0:
            amplitude = jnp.cos(frequency * (instant + 1))
            x_local = offset + jnp.arange(strip, dtype=jnp.int32)
            column_local = (x_local == plane_at).astype(jnp.float32)
            ex, ey, ez, hx, hy, hz = fields
            ez = ez + (amplitude * column_local[None, :, None]) * port_mode[None, None, :]
            fields = curl_y((ex, ey, ez, hx, hy, hz), COURANT * inverse_cols, 2)
            rounded = jnp.stack(fields).reshape(comps, strip, line_cells).astype(jnp.bfloat16)
            solved = solve_turned(turn_rows(rounded, line_count), inverse)
        else:
            rounded = jnp.stack(fields).astype(jnp.bfloat16)
            solved = line_solve(rounded, inverse)
        solved = solved.reshape(6, planes, strip, line_cells)
        fields = curl_xz(
            tuple(solved[i] for i in range(6)), scaled_held if instant == 0 else scaled_rows, 2, 0
        )
        stacked = jnp.stack(fields).reshape(comps, strip, line_cells)
        if inverse_cols is None:
            stacked = jnp.concatenate([stacked] + bf16_parts(inverse_rows), 0)
        turned = turn_rows(stacked.astype(jnp.bfloat16), line_count)
        if inverse_cols is None:
            width = eps_planes * strip
            pieces = [
                turned[:, comps * strip + k * width : comps * strip + (k + 1) * width].astype(jnp.float32)
                for k in range(2)
            ]
            joined = pieces[0] + pieces[1]
            inverse_cols = joined.T.reshape(eps_planes, strip, line_cells)
            turned = turned[:, : comps * strip]
        solved = solve_turned(turned, inverse_held if instant == 0 else inverse)
        solved = solved.reshape(6, planes, strip, line_cells)
        fields = tuple(solved[i] for i in range(6))
        snapshot = fwd_e[instant].astype(jnp.float32)
        intersection = fields[0] * snapshot[0] + fields[1] * snapshot[1] + fields[2] * snapshot[2]
        gradient = gradient + mask_weight * intersection * (inverse_cols * inverse_cols)
    out = jnp.stack(fields)
    return (out[:3], out[3:], gradient)


def solution(mesh):
    in_specs = (
        P(None, "exc", "line", None),
        P(None, "exc", "line", None),
        P(None, None, "exc", "line", None),
        P(None, "line", None),
        P(None, "line", None),
        P(),
        P("exc"),
        P("exc"),
        P("exc"),
    )
    out_specs = (P(None, "exc", "line", None), P(None, "exc", "line", None), P("exc", "line", None))
    return jax.shard_map(
        per_device, mesh=mesh, in_specs=in_specs, out_specs=out_specs, check_vma=False
    )
```

```python
import jax
import jax.numpy as jnp
from jax import lax
from jax.sharding import PartitionSpec as P

COURANT = 0.4


def line_solve(rounded, inverse):
    flattened = rounded.reshape(-1, rounded.shape[-1])
    solved = lax.dot_general(
        flattened, inverse, (((1,), (1,)), ((), ())), preferred_element_type=jnp.float32
    )
    return solved.reshape(rounded.shape)


def turn_rows(block, line_count):
    comps, strip, cells = block.shape
    parts = block.reshape(comps, strip, line_count, strip)
    parts = jnp.transpose(parts, (2, 1, 0, 3)).reshape(line_count, strip, comps * strip)
    parts = lax.all_to_all(parts, "line", 0, 0, tiled=True)
    return parts.reshape(line_count * strip, comps * strip)


def solve_turned(turned, inverse):
    return lax.dot_general(
        turned, inverse, (((0,), (1,)), ((), ())), preferred_element_type=jnp.float32
    )


def bf16_parts(values):
    high = lax.reduce_precision(values, exponent_bits=8, mantissa_bits=7)
    return [high, values - high]


def shift_down(f, along, first):
    inner = f.shape[along]
    return jnp.concatenate([first, lax.slice_in_dim(f, 0, inner - 1, axis=along)], axis=along)


def shift_up(f, along, last):
    inner = f.shape[along]
    return jnp.concatenate([lax.slice_in_dim(f, 1, inner, axis=along), last], axis=along)


def zeros_like_slice(f, along):
    shape = list(f.shape)
    shape[along] = 1
    return jnp.zeros(shape, f.dtype)


def curl_y(fields, scaled, along, below=None, above=None):
    ex, ey, ez, hx, hy, hz = fields
    if below is None:
        below = (zeros_like_slice(hx, along), zeros_like_slice(hz, along))
    if above is None:
        z = zeros_like_slice(hx, along)
        above = (z, z, z, z, z)
    hx_prev = shift_down(hx, along, below[0])
    hz_prev = shift_down(hz, along, below[1])
    ex = ex + scaled * (hz - hz_prev)
    ez = ez - scaled * (hx - hx_prev)
    last = lax.slice_in_dim(hx, hx.shape[along] - 1, hx.shape[along], axis=along)
    last_z = lax.slice_in_dim(hz, hz.shape[along] - 1, hz.shape[along], axis=along)
    ex_a, ez_a, hx_a, hz_a, scaled_a = above
    ex_next_edge = ex_a + scaled_a * (hz_a - last_z)
    ez_next_edge = ez_a - scaled_a * (hx_a - last)
    ex_next = shift_up(ex, along, ex_next_edge)
    ez_next = shift_up(ez, along, ez_next_edge)
    hx = hx - COURANT * (ez_next - ez)
    hz = hz + COURANT * (ex_next - ex)
    return (ex, ey, ez, hx, hy, hz)


def curl_xz(fields, scaled, along_x, along_z):
    ex, ey, ez, hx, hy, hz = fields

    def lower(f, along):
        return f - shift_down(f, along, zeros_like_slice(f, along))

    def upper(f, along):
        return shift_up(f, along, zeros_like_slice(f, along)) - f

    ex = ex - scaled * lower(hy, along_z)
    ey = ey + scaled * (lower(hx, along_z) - lower(hz, along_x))
    ez = ez + scaled * lower(hy, along_x)
    hx = hx + COURANT * upper(ey, along_z)
    hy = hy + COURANT * (upper(ez, along_x) - upper(ex, along_z))
    hz = hz - COURANT * upper(ey, along_x)
    return (ex, ey, ez, hx, hy, hz)


def per_device(
    adj_e, adj_h, fwd_e, permittivity, design_mask, inverse, omega, port_mode, port_plane
):
    line_cells = inverse.shape[0]
    strip = adj_e.shape[2]
    planes = adj_e.shape[1]
    eps_planes = permittivity.shape[0]
    step_count = fwd_e.shape[0]
    line_count = lax.axis_size("line")
    index = lax.axis_index("line")
    offset = index * strip
    inverse_rows = 1.0 / permittivity
    scaled_rows = COURANT * inverse_rows
    frequency = omega[0]
    plane_at = port_plane[0]
    mask_weight = design_mask.astype(jnp.float32)
    gradient = jnp.zeros(design_mask.shape, jnp.float32)
    comps = 6 * planes

    ring = [(i, (i + 1) % line_count) for i in range(line_count)]
    eps_planes_b = jnp.broadcast_to(permittivity, adj_e[0].shape)
    message = jnp.concatenate(
        [adj_e[:, :, -1:], adj_h[:, :, -1:], eps_planes_b[None, :, -1:], adj_h[::2, :, -2:-1]], 0
    )
    message = lax.ppermute(message, "line", ring)
    is_first = index == 0
    column = (jnp.arange(line_cells, dtype=jnp.int32) == plane_at).astype(jnp.float32)
    profile_rows = lax.dynamic_slice_in_dim(port_mode, offset, strip)
    amplitude = jnp.cos(frequency * 1.0)
    ex, ey, ez = adj_e[0], adj_e[1], adj_e[2]
    hx, hy, hz = adj_h[0], adj_h[1], adj_h[2]
    ez = ez + (amplitude * profile_rows[None, :, None]) * column[None, None, :]
    ex1 = ex[:, 1:] + scaled_rows[:, 1:] * (hz[:, 1:] - hz[:, :-1])
    ez1 = ez[:, 1:] - scaled_rows[:, 1:] * (hx[:, 1:] - hx[:, :-1])
    hx1 = hx[:, 1:-1] - COURANT * (ez1[:, 1:] - ez1[:, :-1])
    hz1 = hz[:, 1:-1] + COURANT * (ex1[:, 1:] - ex1[:, :-1])
    inner = (ex1[:, :-1], ey[:, 1:-1], ez1[:, :-1], hx1, hy[:, 1:-1], hz1)
    inner_solved = line_solve(jnp.stack(inner).astype(jnp.bfloat16), inverse)
    inner_fields = curl_xz(tuple(inner_solved[i] for i in range(6)), scaled_rows[:, 1:-1], 2, 0)
    p_ex, p_ey, p_ez, p_hx, p_hy, p_hz = (message[i] for i in range(6))
    p_eps, p_hx2, p_hz2 = message[6], message[7], message[8]
    row_before = (offset + line_cells - 1) % line_cells
    profile_before = lax.dynamic_slice_in_dim(port_mode, row_before, 1)
    p_ez = p_ez + (amplitude * profile_before[None, :, None]) * column[None, None, :]
    p_r = COURANT * (1.0 / p_eps)
    zero_row = jnp.zeros_like(p_hx)
    below_hx = jnp.where(is_first, zero_row, p_hx)
    below_hz = jnp.where(is_first, zero_row, p_hz)
    ex_0 = ex[:, :1] + scaled_rows[:, :1] * (hz[:, :1] - below_hz)
    ez_0 = ez[:, :1] - scaled_rows[:, :1] * (hx[:, :1] - below_hx)
    hx_0 = hx[:, :1] - COURANT * (ez1[:, :1] - ez_0)
    hz_0 = hz[:, :1] + COURANT * (ex1[:, :1] - ex_0)
    ex_y = p_ex + p_r * (p_hz - p_hz2)
    ez_y = p_ez - p_r * (p_hx - p_hx2)
    ex_next = jnp.where(is_first, zero_row, ex_0)
    ez_next = jnp.where(is_first, zero_row, ez_0)
    hx_y = p_hx - COURANT * (ez_next - ez_y)
    hz_y = p_hz + COURANT * (ex_next - ex_y)
    edge = (
        jnp.concatenate([ex_y, ex_0], 1),
        jnp.concatenate([p_ey, ey[:, :1]], 1),
        jnp.concatenate([ez_y, ez_0], 1),
        jnp.concatenate([hx_y, hx_0], 1),
        jnp.concatenate([p_hy, hy[:, :1]], 1),
        jnp.concatenate([hz_y, hz_0], 1),
    )
    edge_solved = line_solve(jnp.stack(edge).astype(jnp.bfloat16), inverse)
    scaled_edge = jnp.concatenate([p_r[:eps_planes], scaled_rows[:, :1]], 1)
    edge_fields = curl_xz(tuple(edge_solved[i] for i in range(6)), scaled_edge, 2, 0)
    first_fields = tuple(jnp.concatenate([a, b], 1) for a, b in zip(edge_fields, inner_fields))
    inverse_held = jnp.roll(inverse, 1, axis=1)
    inverse_cols = None
    for instant in range(step_count):
        if instant > 0:
            amplitude = jnp.cos(frequency * (instant + 1))
            x_local = offset + jnp.arange(strip, dtype=jnp.int32)
            column_local = (x_local == plane_at).astype(jnp.float32)
            ex, ey, ez, hx, hy, hz = fields
            ez = ez + (amplitude * column_local[None, :, None]) * port_mode[None, None, :]
            fields = curl_y((ex, ey, ez, hx, hy, hz), COURANT * inverse_cols, 2)
            rounded = jnp.stack(fields).reshape(comps, strip, line_cells).astype(jnp.bfloat16)
            solved = solve_turned(turn_rows(rounded, line_count), inverse)
            solved = solved.reshape(6, planes, strip, line_cells)
            fields = curl_xz(tuple(solved[i] for i in range(6)), scaled_rows, 2, 0)
        else:
            fields = first_fields
        stacked = jnp.stack(fields).reshape(comps, strip, line_cells)
        if inverse_cols is None:
            stacked = jnp.concatenate([stacked] + bf16_parts(inverse_rows), 0)
        turned = turn_rows(stacked.astype(jnp.bfloat16), line_count)
        if inverse_cols is None:
            width = eps_planes * strip
            pieces = [
                turned[:, comps * strip + k * width : comps * strip + (k + 1) * width].astype(jnp.float32)
                for k in range(2)
            ]
            joined = pieces[0] + pieces[1]
            inverse_cols = joined.T.reshape(eps_planes, strip, line_cells)
            turned = turned[:, : comps * strip]
        solved = solve_turned(turned, inverse_held if instant == 0 else inverse)
        solved = solved.reshape(6, planes, strip, line_cells)
        fields = tuple(solved[i] for i in range(6))
        snapshot = fwd_e[instant].astype(jnp.float32)
        intersection = fields[0] * snapshot[0] + fields[1] * snapshot[1] + fields[2] * snapshot[2]
        gradient = gradient + mask_weight * intersection * (inverse_cols * inverse_cols)
    out = jnp.stack(fields)
    return (out[:3], out[3:], gradient)


def solution(mesh):
    in_specs = (
        P(None, "exc", "line", None),
        P(None, "exc", "line", None),
        P(None, None, "exc", "line", None),
        P(None, "line", None),
        P(None, "line", None),
        P(),
        P("exc"),
        P("exc"),
        P("exc"),
    )
    out_specs = (P(None, "exc", "line", None), P(None, "exc", "line", None), P("exc", "line", None))
    return jax.shard_map(
        per_device, mesh=mesh, in_specs=in_specs, out_specs=out_specs, check_vma=False
    )
```

```python
import jax
import jax.numpy as jnp
from jax import lax
from jax.sharding import PartitionSpec as P

COURANT = 0.4


def line_solve(rounded, inverse):
    flattened = rounded.reshape(-1, rounded.shape[-1])
    solved = lax.dot_general(
        flattened, inverse, (((1,), (1,)), ((), ())), preferred_element_type=jnp.float32
    )
    return solved.reshape(rounded.shape)


def pack_rows(block, line_count):
    comps, rows, cells = block.shape
    strip = cells // line_count
    parts = block.reshape(comps, rows, line_count, strip)
    return jnp.transpose(parts, (2, 1, 0, 3)).reshape(line_count, rows, comps * strip)


def send_rows(parts):
    line_count, strip, width = parts.shape
    parts = lax.all_to_all(parts, "line", 0, 0, tiled=True)
    return parts.reshape(line_count * strip, width)


def turn_rows(block, line_count):
    return send_rows(pack_rows(block, line_count))


def solve_turned(turned, inverse):
    return lax.dot_general(
        turned, inverse, (((0,), (1,)), ((), ())), preferred_element_type=jnp.float32
    )


def bf16_parts(values):
    high = lax.reduce_precision(values, exponent_bits=8, mantissa_bits=7)
    return [high, values - high]


def shift_down(f, along, first):
    inner = f.shape[along]
    return jnp.concatenate([first, lax.slice_in_dim(f, 0, inner - 1, axis=along)], axis=along)


def shift_up(f, along, last):
    inner = f.shape[along]
    return jnp.concatenate([lax.slice_in_dim(f, 1, inner, axis=along), last], axis=along)


def zeros_like_slice(f, along):
    shape = list(f.shape)
    shape[along] = 1
    return jnp.zeros(shape, f.dtype)


def curl_y(fields, scaled, along, below=None, above=None):
    ex, ey, ez, hx, hy, hz = fields
    if below is None:
        below = (zeros_like_slice(hx, along), zeros_like_slice(hz, along))
    if above is None:
        z = zeros_like_slice(hx, along)
        above = (z, z, z, z, z)
    hx_prev = shift_down(hx, along, below[0])
    hz_prev = shift_down(hz, along, below[1])
    ex = ex + scaled * (hz - hz_prev)
    ez = ez - scaled * (hx - hx_prev)
    last = lax.slice_in_dim(hx, hx.shape[along] - 1, hx.shape[along], axis=along)
    last_z = lax.slice_in_dim(hz, hz.shape[along] - 1, hz.shape[along], axis=along)
    ex_a, ez_a, hx_a, hz_a, scaled_a = above
    ex_next_edge = ex_a + scaled_a * (hz_a - last_z)
    ez_next_edge = ez_a - scaled_a * (hx_a - last)
    ex_next = shift_up(ex, along, ex_next_edge)
    ez_next = shift_up(ez, along, ez_next_edge)
    hx = hx - COURANT * (ez_next - ez)
    hz = hz + COURANT * (ex_next - ex)
    return (ex, ey, ez, hx, hy, hz)


def curl_xz(fields, scaled, along_x, along_z):
    ex, ey, ez, hx, hy, hz = fields

    def lower(f, along):
        return f - shift_down(f, along, zeros_like_slice(f, along))

    def upper(f, along):
        return shift_up(f, along, zeros_like_slice(f, along)) - f

    ex = ex - scaled * lower(hy, along_z)
    ey = ey + scaled * (lower(hx, along_z) - lower(hz, along_x))
    ez = ez + scaled * lower(hy, along_x)
    hx = hx + COURANT * upper(ey, along_z)
    hy = hy + COURANT * (upper(ez, along_x) - upper(ex, along_z))
    hz = hz - COURANT * upper(ey, along_x)
    return (ex, ey, ez, hx, hy, hz)


def per_device(
    adj_e, adj_h, fwd_e, permittivity, design_mask, inverse, omega, port_mode, port_plane
):
    line_cells = inverse.shape[0]
    strip = adj_e.shape[2]
    planes = adj_e.shape[1]
    eps_planes = permittivity.shape[0]
    step_count = fwd_e.shape[0]
    line_count = lax.axis_size("line")
    index = lax.axis_index("line")
    offset = index * strip
    inverse_rows = 1.0 / permittivity
    scaled_rows = COURANT * inverse_rows
    frequency = omega[0]
    plane_at = port_plane[0]
    mask_weight = design_mask.astype(jnp.float32)
    gradient = jnp.zeros(design_mask.shape, jnp.float32)
    comps = 6 * planes

    ring = [(i, (i + 1) % line_count) for i in range(line_count)]
    eps_planes_b = jnp.broadcast_to(permittivity, adj_e[0].shape)
    message = jnp.concatenate(
        [adj_e[:, :, -1:], adj_h[:, :, -1:], eps_planes_b[None, :, -1:], adj_h[::2, :, -2:-1]], 0
    )
    message = lax.ppermute(message, "line", ring)
    is_first = index == 0
    column = (jnp.arange(line_cells, dtype=jnp.int32) == plane_at).astype(jnp.float32)
    profile_rows = lax.dynamic_slice_in_dim(port_mode, offset, strip)
    amplitude = jnp.cos(frequency * 1.0)
    ex, ey, ez = adj_e[0], adj_e[1], adj_e[2]
    hx, hy, hz = adj_h[0], adj_h[1], adj_h[2]
    ez = ez + (amplitude * profile_rows[None, :, None]) * column[None, None, :]
    ex1 = ex[:, 1:] + scaled_rows[:, 1:] * (hz[:, 1:] - hz[:, :-1])
    ez1 = ez[:, 1:] - scaled_rows[:, 1:] * (hx[:, 1:] - hx[:, :-1])
    hx1 = hx[:, 1:-1] - COURANT * (ez1[:, 1:] - ez1[:, :-1])
    hz1 = hz[:, 1:-1] + COURANT * (ex1[:, 1:] - ex1[:, :-1])
    inner = (ex1[:, :-1], ey[:, 1:-1], ez1[:, :-1], hx1, hy[:, 1:-1], hz1)
    inner_solved = line_solve(jnp.stack(inner).astype(jnp.bfloat16), inverse)
    inner_fields = curl_xz(tuple(inner_solved[i] for i in range(6)), scaled_rows[:, 1:-1], 2, 0)
    p_ex, p_ey, p_ez, p_hx, p_hy, p_hz = (message[i] for i in range(6))
    p_eps, p_hx2, p_hz2 = message[6], message[7], message[8]
    row_before = (offset + line_cells - 1) % line_cells
    profile_before = lax.dynamic_slice_in_dim(port_mode, row_before, 1)
    p_ez = p_ez + (amplitude * profile_before[None, :, None]) * column[None, None, :]
    p_r = COURANT * (1.0 / p_eps)
    zero_row = jnp.zeros_like(p_hx)
    below_hx = jnp.where(is_first, zero_row, p_hx)
    below_hz = jnp.where(is_first, zero_row, p_hz)
    ex_0 = ex[:, :1] + scaled_rows[:, :1] * (hz[:, :1] - below_hz)
    ez_0 = ez[:, :1] - scaled_rows[:, :1] * (hx[:, :1] - below_hx)
    hx_0 = hx[:, :1] - COURANT * (ez1[:, :1] - ez_0)
    hz_0 = hz[:, :1] + COURANT * (ex1[:, :1] - ex_0)
    ex_y = p_ex + p_r * (p_hz - p_hz2)
    ez_y = p_ez - p_r * (p_hx - p_hx2)
    ex_next = jnp.where(is_first, zero_row, ex_0)
    ez_next = jnp.where(is_first, zero_row, ez_0)
    hx_y = p_hx - COURANT * (ez_next - ez_y)
    hz_y = p_hz + COURANT * (ex_next - ex_y)
    edge = (
        jnp.concatenate([ex_y, ex_0], 1),
        jnp.concatenate([p_ey, ey[:, :1]], 1),
        jnp.concatenate([ez_y, ez_0], 1),
        jnp.concatenate([hx_y, hx_0], 1),
        jnp.concatenate([p_hy, hy[:, :1]], 1),
        jnp.concatenate([hz_y, hz_0], 1),
    )
    edge_solved = line_solve(jnp.stack(edge).astype(jnp.bfloat16), inverse)
    scaled_edge = jnp.concatenate([p_r[:eps_planes], scaled_rows[:, :1]], 1)
    edge_fields = curl_xz(tuple(edge_solved[i] for i in range(6)), scaled_edge, 2, 0)
    def packed(fields, eps_rows):
        stacked = jnp.stack(fields).reshape((comps,) + fields[0].shape[1:])
        stacked = jnp.concatenate([stacked] + bf16_parts(eps_rows), 0)
        return pack_rows(stacked.astype(jnp.bfloat16), line_count)

    first_parts = jnp.concatenate(
        [packed(edge_fields, inverse_rows[:, :2]), packed(inner_fields, inverse_rows[:, 2:])], 1
    )
    inverse_held = jnp.roll(inverse, 1, axis=1)
    inverse_cols = None
    for instant in range(step_count):
        if instant > 0:
            amplitude = jnp.cos(frequency * (instant + 1))
            x_local = offset + jnp.arange(strip, dtype=jnp.int32)
            column_local = (x_local == plane_at).astype(jnp.float32)
            ex, ey, ez, hx, hy, hz = fields
            ez = ez + (amplitude * column_local[None, :, None]) * port_mode[None, None, :]
            fields = curl_y((ex, ey, ez, hx, hy, hz), COURANT * inverse_cols, 2)
            rounded = jnp.stack(fields).reshape(comps, strip, line_cells).astype(jnp.bfloat16)
            solved = solve_turned(turn_rows(rounded, line_count), inverse)
            solved = solved.reshape(6, planes, strip, line_cells)
            fields = curl_xz(tuple(solved[i] for i in range(6)), scaled_rows, 2, 0)
            stacked = jnp.stack(fields).reshape(comps, strip, line_cells)
            turned = turn_rows(stacked.astype(jnp.bfloat16), line_count)
        else:
            turned = send_rows(first_parts)
        if inverse_cols is None:
            width = eps_planes * strip
            pieces = [
                turned[:, comps * strip + k * width : comps * strip + (k + 1) * width].astype(jnp.float32)
                for k in range(2)
            ]
            joined = pieces[0] + pieces[1]
            inverse_cols = joined.T.reshape(eps_planes, strip, line_cells)
            turned = turned[:, : comps * strip]
        held = inverse_held if instant == 0 else inverse
        half = 3 * planes * strip
        solved_e = solve_turned(turned[:, :half], held).reshape(3, planes, strip, line_cells)
        solved_h = solve_turned(turned[:, half:], held).reshape(3, planes, strip, line_cells)
        fields = tuple(solved_e[i] for i in range(3)) + tuple(solved_h[i] for i in range(3))
        snapshot = fwd_e[instant].astype(jnp.float32)
        intersection = fields[0] * snapshot[0] + fields[1] * snapshot[1] + fields[2] * snapshot[2]
        gradient = gradient + mask_weight * intersection * (inverse_cols * inverse_cols)
    return (solved_e, solved_h, gradient)


def solution(mesh):
    in_specs = (
        P(None, "exc", "line", None),
        P(None, "exc", "line", None),
        P(None, None, "exc", "line", None),
        P(None, "line", None),
        P(None, "line", None),
        P(),
        P("exc"),
        P("exc"),
        P("exc"),
    )
    out_specs = (P(None, "exc", "line", None), P(None, "exc", "line", None), P("exc", "line", None))
    return jax.shard_map(
        per_device, mesh=mesh, in_specs=in_specs, out_specs=out_specs, check_vma=False
    )
```

```python
import jax
import jax.numpy as jnp
from jax import lax
from jax.sharding import PartitionSpec as P
from jax.experimental import pallas as pl

COURANT = 0.4


def line_solve(rounded, inverse):
    flattened = rounded.reshape(-1, rounded.shape[-1])
    solved = lax.dot_general(
        flattened, inverse, (((1,), (1,)), ((), ())), preferred_element_type=jnp.float32
    )
    return solved.reshape(rounded.shape)


def _pack_kernel(x_ref, o_ref):
    comps = x_ref.shape[0]
    blocks = o_ref.shape[0]
    width = o_ref.shape[2] // comps
    for c in range(comps):
        values = x_ref[c]
        for e in range(blocks):
            o_ref[e, :, c * width : (c + 1) * width] = values[:, e * width : (e + 1) * width]


def turn_rows(block, line_count):
    comps, strip, cells = block.shape
    width = cells // line_count
    parts = pl.pallas_call(
        _pack_kernel,
        out_shape=jax.ShapeDtypeStruct((line_count, strip, comps * width), block.dtype),
    )(block)
    parts = lax.all_to_all(parts.astype(jnp.bfloat16), "line", 0, 0, tiled=True)
    return parts.reshape(line_count * strip, comps * width)


def solve_turned(turned, inverse):
    return lax.dot_general(
        turned, inverse, (((0,), (1,)), ((), ())), preferred_element_type=jnp.float32
    )


def bf16_parts(values):
    high = lax.reduce_precision(values, exponent_bits=8, mantissa_bits=7)
    return [high, values - high]


def shift_down(f, along, first):
    inner = f.shape[along]
    return jnp.concatenate([first, lax.slice_in_dim(f, 0, inner - 1, axis=along)], axis=along)


def shift_up(f, along, last):
    inner = f.shape[along]
    return jnp.concatenate([lax.slice_in_dim(f, 1, inner, axis=along), last], axis=along)


def zeros_like_slice(f, along):
    shape = list(f.shape)
    shape[along] = 1
    return jnp.zeros(shape, f.dtype)


def curl_y(fields, scaled, along, below=None, above=None):
    ex, ey, ez, hx, hy, hz = fields
    if below is None:
        below = (zeros_like_slice(hx, along), zeros_like_slice(hz, along))
    if above is None:
        z = zeros_like_slice(hx, along)
        above = (z, z, z, z, z)
    hx_prev = shift_down(hx, along, below[0])
    hz_prev = shift_down(hz, along, below[1])
    ex = ex + scaled * (hz - hz_prev)
    ez = ez - scaled * (hx - hx_prev)
    last = lax.slice_in_dim(hx, hx.shape[along] - 1, hx.shape[along], axis=along)
    last_z = lax.slice_in_dim(hz, hz.shape[along] - 1, hz.shape[along], axis=along)
    ex_a, ez_a, hx_a, hz_a, scaled_a = above
    ex_next_edge = ex_a + scaled_a * (hz_a - last_z)
    ez_next_edge = ez_a - scaled_a * (hx_a - last)
    ex_next = shift_up(ex, along, ex_next_edge)
    ez_next = shift_up(ez, along, ez_next_edge)
    hx = hx - COURANT * (ez_next - ez)
    hz = hz + COURANT * (ex_next - ex)
    return (ex, ey, ez, hx, hy, hz)


def curl_xz(fields, scaled, along_x, along_z):
    ex, ey, ez, hx, hy, hz = fields

    def lower(f, along):
        return f - shift_down(f, along, zeros_like_slice(f, along))

    def upper(f, along):
        return shift_up(f, along, zeros_like_slice(f, along)) - f

    ex = ex - scaled * lower(hy, along_z)
    ey = ey + scaled * (lower(hx, along_z) - lower(hz, along_x))
    ez = ez + scaled * lower(hy, along_x)
    hx = hx + COURANT * upper(ey, along_z)
    hy = hy + COURANT * (upper(ez, along_x) - upper(ex, along_z))
    hz = hz - COURANT * upper(ey, along_x)
    return (ex, ey, ez, hx, hy, hz)


def per_device(
    adj_e, adj_h, fwd_e, permittivity, design_mask, inverse, omega, port_mode, port_plane
):
    line_cells = inverse.shape[0]
    strip = adj_e.shape[2]
    planes = adj_e.shape[1]
    eps_planes = permittivity.shape[0]
    step_count = fwd_e.shape[0]
    line_count = lax.axis_size("line")
    index = lax.axis_index("line")
    offset = index * strip
    inverse_rows = 1.0 / permittivity
    scaled_rows = COURANT * inverse_rows
    frequency = omega[0]
    plane_at = port_plane[0]
    mask_weight = design_mask.astype(jnp.float32)
    gradient = jnp.zeros(design_mask.shape, jnp.float32)
    comps = 6 * planes

    column = (jnp.arange(line_cells, dtype=jnp.int32) == plane_at).astype(jnp.float32)
    profile_rows = lax.dynamic_slice_in_dim(port_mode, offset, strip)
    amplitude = jnp.cos(frequency * 1.0)
    ex, ey, ez = adj_e[0], adj_e[1], adj_e[2]
    hx, hy, hz = adj_h[0], adj_h[1], adj_h[2]
    ez = ez + (amplitude * profile_rows[None, :, None]) * column[None, None, :]
    is_first = index == 0
    ring = [(i, (i + 1) % line_count) for i in range(line_count)]
    scaled_planes = jnp.broadcast_to(scaled_rows, ex.shape)
    message = jnp.stack(
        [f[:, -1:] for f in (ex, ey, ez, hx, hy, hz, scaled_planes)] + [hx[:, -2:-1], hz[:, -2:-1]]
    )
    message = lax.ppermute(message, "line", ring)
    p_ex, p_ey, p_ez, p_hx, p_hy, p_hz, p_r, p_hx2, p_hz2 = (message[i] for i in range(9))
    zero_row = jnp.zeros_like(p_hx)
    hx_prev = shift_down(hx, 1, jnp.where(is_first, zero_row, p_hx))
    hz_prev = shift_down(hz, 1, jnp.where(is_first, zero_row, p_hz))
    ex1 = ex + scaled_rows * (hz - hz_prev)
    ez1 = ez - scaled_rows * (hx - hx_prev)
    hx1 = hx[:, :-1] - COURANT * (ez1[:, 1:] - ez1[:, :-1])
    hz1 = hz[:, :-1] + COURANT * (ex1[:, 1:] - ex1[:, :-1])
    ex_y = p_ex + p_r * (p_hz - p_hz2)
    ez_y = p_ez - p_r * (p_hx - p_hx2)
    ex_next = jnp.where(is_first, zero_row, ex1[:, :1])
    ez_next = jnp.where(is_first, zero_row, ez1[:, :1])
    hx_y = p_hx - COURANT * (ez_next - ez_y)
    hz_y = p_hz + COURANT * (ex_next - ex_y)
    fields = (
        jnp.concatenate([ex_y, ex1[:, :-1]], 1),
        jnp.concatenate([p_ey, ey[:, :-1]], 1),
        jnp.concatenate([ez_y, ez1[:, :-1]], 1),
        jnp.concatenate([hx_y, hx1], 1),
        jnp.concatenate([p_hy, hy[:, :-1]], 1),
        jnp.concatenate([hz_y, hz1], 1),
    )
    scaled_held = jnp.concatenate([p_r[:eps_planes], scaled_rows[:, :-1]], 1)
    inverse_held = jnp.roll(inverse, 1, axis=1)
    inverse_cols = None
    for instant in range(step_count):
        if instant > 0:
            amplitude = jnp.cos(frequency * (instant + 1))
            x_local = offset + jnp.arange(strip, dtype=jnp.int32)
            column_local = (x_local == plane_at).astype(jnp.float32)
            ex, ey, ez, hx, hy, hz = fields
            ez = ez + (amplitude * column_local[None, :, None]) * port_mode[None, None, :]
            fields = curl_y((ex, ey, ez, hx, hy, hz), COURANT * inverse_cols, 2)
            rounded = jnp.stack(fields).reshape(comps, strip, line_cells)
            solved = solve_turned(turn_rows(rounded, line_count), inverse)
        else:
            rounded = jnp.stack(fields).astype(jnp.bfloat16)
            solved = line_solve(rounded, inverse)
        solved = solved.reshape(6, planes, strip, line_cells)
        fields = curl_xz(
            tuple(solved[i] for i in range(6)), scaled_held if instant == 0 else scaled_rows, 2, 0
        )
        stacked = jnp.stack(fields).reshape(comps, strip, line_cells)
        if inverse_cols is None:
            stacked = jnp.concatenate([stacked] + bf16_parts(inverse_rows), 0)
        turned = turn_rows(stacked, line_count)
        if inverse_cols is None:
            width = eps_planes * strip
            pieces = [
                turned[:, comps * strip + k * width : comps * strip + (k + 1) * width].astype(jnp.float32)
                for k in range(2)
            ]
            joined = pieces[0] + pieces[1]
            inverse_cols = joined.T.reshape(eps_planes, strip, line_cells)
            turned = turned[:, : comps * strip]
        solved = solve_turned(turned, inverse_held if instant == 0 else inverse)
        solved = solved.reshape(6, planes, strip, line_cells)
        fields = tuple(solved[i] for i in range(6))
        snapshot = fwd_e[instant].astype(jnp.float32)
        intersection = fields[0] * snapshot[0] + fields[1] * snapshot[1] + fields[2] * snapshot[2]
        gradient = gradient + mask_weight * intersection * (inverse_cols * inverse_cols)
    out = jnp.stack(fields)
    return (out[:3], out[3:], gradient)


def solution(mesh):
    in_specs = (
        P(None, "exc", "line", None),
        P(None, "exc", "line", None),
        P(None, None, "exc", "line", None),
        P(None, "line", None),
        P(None, "line", None),
        P(),
        P("exc"),
        P("exc"),
        P("exc"),
    )
    out_specs = (P(None, "exc", "line", None), P(None, "exc", "line", None), P("exc", "line", None))
    return jax.shard_map(
        per_device, mesh=mesh, in_specs=in_specs, out_specs=out_specs, check_vma=False
    )
```

```python
import jax
import jax.numpy as jnp
from jax import lax
from jax.sharding import PartitionSpec as P

COURANT = 0.4


def line_solve(rounded, inverse):
    flattened = rounded.reshape(-1, rounded.shape[-1])
    solved = lax.dot_general(
        flattened, inverse, (((1,), (1,)), ((), ())), preferred_element_type=jnp.float32
    )
    return solved.reshape(rounded.shape)


def turn_rows(block, line_count):
    comps, strip, cells = block.shape
    parts = block.reshape(comps, strip, line_count, strip)
    parts = jnp.transpose(parts, (2, 1, 0, 3)).reshape(line_count, strip, comps * strip)
    parts = lax.all_to_all(parts, "line", 0, 0, tiled=True)
    return parts.reshape(line_count * strip, comps * strip)


def solve_turned(turned, inverse):
    return lax.dot_general(
        turned, inverse, (((0,), (1,)), ((), ())), preferred_element_type=jnp.float32
    )


def bf16_parts(values):
    high = lax.reduce_precision(values, exponent_bits=8, mantissa_bits=7)
    return [high, values - high]


def shift_down(f, along, first):
    inner = f.shape[along]
    return jnp.concatenate([first, lax.slice_in_dim(f, 0, inner - 1, axis=along)], axis=along)


def shift_up(f, along, last):
    inner = f.shape[along]
    return jnp.concatenate([lax.slice_in_dim(f, 1, inner, axis=along), last], axis=along)


def zeros_like_slice(f, along):
    shape = list(f.shape)
    shape[along] = 1
    return jnp.zeros(shape, f.dtype)


def curl_y(fields, scaled, along, below=None, above=None):
    ex, ey, ez, hx, hy, hz = fields
    if below is None:
        below = (zeros_like_slice(hx, along), zeros_like_slice(hz, along))
    if above is None:
        z = zeros_like_slice(hx, along)
        above = (z, z, z, z, z)
    hx_prev = shift_down(hx, along, below[0])
    hz_prev = shift_down(hz, along, below[1])
    ex = ex + scaled * (hz - hz_prev)
    ez = ez - scaled * (hx - hx_prev)
    last = lax.slice_in_dim(hx, hx.shape[along] - 1, hx.shape[along], axis=along)
    last_z = lax.slice_in_dim(hz, hz.shape[along] - 1, hz.shape[along], axis=along)
    ex_a, ez_a, hx_a, hz_a, scaled_a = above
    ex_next_edge = ex_a + scaled_a * (hz_a - last_z)
    ez_next_edge = ez_a - scaled_a * (hx_a - last)
    ex_next = shift_up(ex, along, ex_next_edge)
    ez_next = shift_up(ez, along, ez_next_edge)
    hx = hx - COURANT * (ez_next - ez)
    hz = hz + COURANT * (ex_next - ex)
    return (ex, ey, ez, hx, hy, hz)


def curl_xz(fields, scaled, along_x, along_z):
    ex, ey, ez, hx, hy, hz = fields

    def lower(f, along):
        return f - shift_down(f, along, zeros_like_slice(f, along))

    def upper(f, along):
        return shift_up(f, along, zeros_like_slice(f, along)) - f

    ex = ex - scaled * lower(hy, along_z)
    ey = ey + scaled * (lower(hx, along_z) - lower(hz, along_x))
    ez = ez + scaled * lower(hy, along_x)
    hx = hx + COURANT * upper(ey, along_z)
    hy = hy + COURANT * (upper(ez, along_x) - upper(ex, along_z))
    hz = hz - COURANT * upper(ey, along_x)
    return (ex, ey, ez, hx, hy, hz)


def per_device(
    adj_e, adj_h, fwd_e, permittivity, design_mask, inverse, omega, port_mode, port_plane
):
    line_cells = inverse.shape[0]
    strip = adj_e.shape[2]
    planes = adj_e.shape[1]
    eps_planes = permittivity.shape[0]
    step_count = fwd_e.shape[0]
    line_count = lax.axis_size("line")
    index = lax.axis_index("line")
    offset = index * strip
    inverse_rows = 1.0 / permittivity
    scaled_rows = COURANT * inverse_rows
    frequency = omega[0]
    plane_at = port_plane[0]
    mask_weight = design_mask.astype(jnp.float32)
    gradient = jnp.zeros(design_mask.shape, jnp.float32)
    comps = 6 * planes

    ring = [(i, (i + 1) % line_count) for i in range(line_count)]
    eps_planes_b = jnp.broadcast_to(permittivity, adj_e[0].shape)
    message = jnp.concatenate(
        [adj_e[:, :, -1:], adj_h[:, :, -1:], eps_planes_b[None, :, -1:], adj_h[::2, :, -2:-1]], 0
    )
    message = lax.ppermute(message, "line", ring)
    column = (jnp.arange(line_cells, dtype=jnp.int32) == plane_at).astype(jnp.float32)
    profile_rows = lax.dynamic_slice_in_dim(port_mode, offset, strip)
    amplitude = jnp.cos(frequency * 1.0)
    ex, ey, ez = adj_e[0], adj_e[1], adj_e[2]
    hx, hy, hz = adj_h[0], adj_h[1], adj_h[2]
    ez = ez + (amplitude * profile_rows[None, :, None]) * column[None, None, :]
    is_first = index == 0
    p_ex, p_ey, p_ez, p_hx, p_hy, p_hz = (message[i] for i in range(6))
    p_eps, p_hx2, p_hz2 = message[6], message[7], message[8]
    row_before = (offset + line_cells - 1) % line_cells
    profile_before = lax.dynamic_slice_in_dim(port_mode, row_before, 1)
    p_ez = p_ez + (amplitude * profile_before[None, :, None]) * column[None, None, :]
    p_r = COURANT * (1.0 / p_eps)
    zero_row = jnp.zeros_like(p_hx)
    hx_prev = shift_down(hx, 1, jnp.where(is_first, zero_row, p_hx))
    hz_prev = shift_down(hz, 1, jnp.where(is_first, zero_row, p_hz))
    ex1 = ex + scaled_rows * (hz - hz_prev)
    ez1 = ez - scaled_rows * (hx - hx_prev)
    hx1 = hx[:, :-1] - COURANT * (ez1[:, 1:] - ez1[:, :-1])
    hz1 = hz[:, :-1] + COURANT * (ex1[:, 1:] - ex1[:, :-1])
    ex_y = p_ex + p_r * (p_hz - p_hz2)
    ez_y = p_ez - p_r * (p_hx - p_hx2)
    ex_next = jnp.where(is_first, zero_row, ex1[:, :1])
    ez_next = jnp.where(is_first, zero_row, ez1[:, :1])
    hx_y = p_hx - COURANT * (ez_next - ez_y)
    hz_y = p_hz + COURANT * (ex_next - ex_y)
    fields = (
        jnp.concatenate([ex_y, ex1[:, :-1]], 1),
        jnp.concatenate([p_ey, ey[:, :-1]], 1),
        jnp.concatenate([ez_y, ez1[:, :-1]], 1),
        jnp.concatenate([hx_y, hx1], 1),
        jnp.concatenate([p_hy, hy[:, :-1]], 1),
        jnp.concatenate([hz_y, hz1], 1),
    )
    scaled_held = jnp.concatenate([p_r[:eps_planes], scaled_rows[:, :-1]], 1)
    inverse_held = jnp.roll(inverse, 1, axis=1)
    inverse_cols = None
    for instant in range(step_count):
        if instant > 0:
            amplitude = jnp.cos(frequency * (instant + 1))
            x_local = offset + jnp.arange(strip, dtype=jnp.int32)
            column_local = (x_local == plane_at).astype(jnp.float32)
            ex, ey, ez, hx, hy, hz = fields
            ez = ez + (amplitude * column_local[None, :, None]) * port_mode[None, None, :]
            fields = curl_y((ex, ey, ez, hx, hy, hz), COURANT * inverse_cols, 2)
            rounded = jnp.stack(fields).reshape(comps, strip, line_cells).astype(jnp.bfloat16)
            solved = solve_turned(turn_rows(rounded, line_count), inverse)
        else:
            rounded = jnp.stack(fields).astype(jnp.bfloat16)
            solved = line_solve(rounded, inverse)
        solved = solved.reshape(6, planes, strip, line_cells)
        fields = curl_xz(
            tuple(solved[i] for i in range(6)), scaled_held if instant == 0 else scaled_rows, 2, 0
        )
        stacked = jnp.stack(fields).reshape(comps, strip, line_cells)
        if inverse_cols is None:
            stacked = jnp.concatenate([stacked] + bf16_parts(inverse_rows), 0)
        turned = turn_rows(stacked.astype(jnp.bfloat16), line_count)
        if inverse_cols is None:
            width = eps_planes * strip
            pieces = [
                turned[:, comps * strip + k * width : comps * strip + (k + 1) * width].astype(jnp.float32)
                for k in range(2)
            ]
            joined = pieces[0] + pieces[1]
            inverse_cols = joined.T.reshape(eps_planes, strip, line_cells)
            turned = turned[:, : comps * strip]
        solved = solve_turned(turned, inverse_held if instant == 0 else inverse)
        solved = solved.reshape(6, planes, strip, line_cells)
        fields = tuple(solved[i] for i in range(6))
        snapshot = fwd_e[instant].astype(jnp.float32)
        intersection = fields[0] * snapshot[0] + fields[1] * snapshot[1] + fields[2] * snapshot[2]
        gradient = gradient + mask_weight * intersection * (inverse_cols * inverse_cols)
    out = jnp.stack(fields)
    return (out[:3], out[3:], gradient)


def solution(mesh):
    in_specs = (
        P(None, "exc", "line", None),
        P(None, "exc", "line", None),
        P(None, None, "exc", "line", None),
        P(None, "line", None),
        P(None, "line", None),
        P(),
        P("exc"),
        P("exc"),
        P("exc"),
    )
    out_specs = (P(None, "exc", "line", None), P(None, "exc", "line", None), P("exc", "line", None))
    return jax.shard_map(
        per_device, mesh=mesh, in_specs=in_specs, out_specs=out_specs, check_vma=False
    )
```

```python
import jax
import jax.numpy as jnp
from jax import lax
from jax.sharding import PartitionSpec as P
from jax.experimental.layout import Layout, with_layout_constraint

COURANT = 0.4


def line_solve(rounded, inverse):
    flattened = rounded.reshape(-1, rounded.shape[-1])
    solved = lax.dot_general(
        flattened, inverse, (((1,), (1,)), ((), ())), preferred_element_type=jnp.float32
    )
    return solved.reshape(rounded.shape)


def turn_rows(block, line_count):
    comps, strip, cells = block.shape
    block = with_layout_constraint(block, Layout(major_to_minor=(0, 1, 2)))
    parts = block.reshape(comps, strip, line_count, strip)
    parts = jnp.transpose(parts, (2, 1, 0, 3)).reshape(line_count, strip, comps * strip)
    parts = lax.all_to_all(parts, "line", 0, 0, tiled=True)
    return parts.reshape(line_count * strip, comps * strip)


def solve_turned(turned, inverse):
    return lax.dot_general(
        turned, inverse, (((0,), (1,)), ((), ())), preferred_element_type=jnp.float32
    )


def bf16_parts(values):
    high = lax.reduce_precision(values, exponent_bits=8, mantissa_bits=7)
    return [high, values - high]


def shift_down(f, along, first):
    inner = f.shape[along]
    return jnp.concatenate([first, lax.slice_in_dim(f, 0, inner - 1, axis=along)], axis=along)


def shift_up(f, along, last):
    inner = f.shape[along]
    return jnp.concatenate([lax.slice_in_dim(f, 1, inner, axis=along), last], axis=along)


def zeros_like_slice(f, along):
    shape = list(f.shape)
    shape[along] = 1
    return jnp.zeros(shape, f.dtype)


def curl_y(fields, scaled, along, below=None, above=None):
    ex, ey, ez, hx, hy, hz = fields
    if below is None:
        below = (zeros_like_slice(hx, along), zeros_like_slice(hz, along))
    if above is None:
        z = zeros_like_slice(hx, along)
        above = (z, z, z, z, z)
    hx_prev = shift_down(hx, along, below[0])
    hz_prev = shift_down(hz, along, below[1])
    ex = ex + scaled * (hz - hz_prev)
    ez = ez - scaled * (hx - hx_prev)
    last = lax.slice_in_dim(hx, hx.shape[along] - 1, hx.shape[along], axis=along)
    last_z = lax.slice_in_dim(hz, hz.shape[along] - 1, hz.shape[along], axis=along)
    ex_a, ez_a, hx_a, hz_a, scaled_a = above
    ex_next_edge = ex_a + scaled_a * (hz_a - last_z)
    ez_next_edge = ez_a - scaled_a * (hx_a - last)
    ex_next = shift_up(ex, along, ex_next_edge)
    ez_next = shift_up(ez, along, ez_next_edge)
    hx = hx - COURANT * (ez_next - ez)
    hz = hz + COURANT * (ex_next - ex)
    return (ex, ey, ez, hx, hy, hz)


def curl_xz(fields, scaled, along_x, along_z):
    ex, ey, ez, hx, hy, hz = fields

    def lower(f, along):
        return f - shift_down(f, along, zeros_like_slice(f, along))

    def upper(f, along):
        return shift_up(f, along, zeros_like_slice(f, along)) - f

    ex = ex - scaled * lower(hy, along_z)
    ey = ey + scaled * (lower(hx, along_z) - lower(hz, along_x))
    ez = ez + scaled * lower(hy, along_x)
    hx = hx + COURANT * upper(ey, along_z)
    hy = hy + COURANT * (upper(ez, along_x) - upper(ex, along_z))
    hz = hz - COURANT * upper(ey, along_x)
    return (ex, ey, ez, hx, hy, hz)


def per_device(
    adj_e, adj_h, fwd_e, permittivity, design_mask, inverse, omega, port_mode, port_plane
):
    line_cells = inverse.shape[0]
    strip = adj_e.shape[2]
    planes = adj_e.shape[1]
    eps_planes = permittivity.shape[0]
    step_count = fwd_e.shape[0]
    line_count = lax.axis_size("line")
    index = lax.axis_index("line")
    offset = index * strip
    inverse_rows = 1.0 / permittivity
    scaled_rows = COURANT * inverse_rows
    frequency = omega[0]
    plane_at = port_plane[0]
    mask_weight = design_mask.astype(jnp.float32)
    gradient = jnp.zeros(design_mask.shape, jnp.float32)
    comps = 6 * planes

    column = (jnp.arange(line_cells, dtype=jnp.int32) == plane_at).astype(jnp.float32)
    profile_rows = lax.dynamic_slice_in_dim(port_mode, offset, strip)
    amplitude = jnp.cos(frequency * 1.0)
    ex, ey, ez = adj_e[0], adj_e[1], adj_e[2]
    hx, hy, hz = adj_h[0], adj_h[1], adj_h[2]
    ez = ez + (amplitude * profile_rows[None, :, None]) * column[None, None, :]
    is_first = index == 0
    ring = [(i, (i + 1) % line_count) for i in range(line_count)]
    scaled_planes = jnp.broadcast_to(scaled_rows, ex.shape)
    message = jnp.stack(
        [f[:, -1:] for f in (ex, ey, ez, hx, hy, hz, scaled_planes)] + [hx[:, -2:-1], hz[:, -2:-1]]
    )
    message = lax.ppermute(message, "line", ring)
    p_ex, p_ey, p_ez, p_hx, p_hy, p_hz, p_r, p_hx2, p_hz2 = (message[i] for i in range(9))
    zero_row = jnp.zeros_like(p_hx)
    hx_prev = shift_down(hx, 1, jnp.where(is_first, zero_row, p_hx))
    hz_prev = shift_down(hz, 1, jnp.where(is_first, zero_row, p_hz))
    ex1 = ex + scaled_rows * (hz - hz_prev)
    ez1 = ez - scaled_rows * (hx - hx_prev)
    hx1 = hx[:, :-1] - COURANT * (ez1[:, 1:] - ez1[:, :-1])
    hz1 = hz[:, :-1] + COURANT * (ex1[:, 1:] - ex1[:, :-1])
    ex_y = p_ex + p_r * (p_hz - p_hz2)
    ez_y = p_ez - p_r * (p_hx - p_hx2)
    ex_next = jnp.where(is_first, zero_row, ex1[:, :1])
    ez_next = jnp.where(is_first, zero_row, ez1[:, :1])
    hx_y = p_hx - COURANT * (ez_next - ez_y)
    hz_y = p_hz + COURANT * (ex_next - ex_y)
    fields = (
        jnp.concatenate([ex_y, ex1[:, :-1]], 1),
        jnp.concatenate([p_ey, ey[:, :-1]], 1),
        jnp.concatenate([ez_y, ez1[:, :-1]], 1),
        jnp.concatenate([hx_y, hx1], 1),
        jnp.concatenate([p_hy, hy[:, :-1]], 1),
        jnp.concatenate([hz_y, hz1], 1),
    )
    scaled_held = jnp.concatenate([p_r[:eps_planes], scaled_rows[:, :-1]], 1)
    inverse_held = jnp.roll(inverse, 1, axis=1)
    inverse_cols = None
    for instant in range(step_count):
        if instant > 0:
            amplitude = jnp.cos(frequency * (instant + 1))
            x_local = offset + jnp.arange(strip, dtype=jnp.int32)
            column_local = (x_local == plane_at).astype(jnp.float32)
            ex, ey, ez, hx, hy, hz = fields
            ez = ez + (amplitude * column_local[None, :, None]) * port_mode[None, None, :]
            fields = curl_y((ex, ey, ez, hx, hy, hz), COURANT * inverse_cols, 2)
            rounded = jnp.stack(fields).reshape(comps, strip, line_cells).astype(jnp.bfloat16)
            solved = solve_turned(turn_rows(rounded, line_count), inverse)
        else:
            rounded = jnp.stack(fields).astype(jnp.bfloat16)
            solved = line_solve(rounded, inverse)
        solved = solved.reshape(6, planes, strip, line_cells)
        fields = curl_xz(
            tuple(solved[i] for i in range(6)), scaled_held if instant == 0 else scaled_rows, 2, 0
        )
        stacked = jnp.stack(fields).reshape(comps, strip, line_cells)
        if inverse_cols is None:
            stacked = jnp.concatenate([stacked] + bf16_parts(inverse_rows), 0)
        turned = turn_rows(stacked.astype(jnp.bfloat16), line_count)
        if inverse_cols is None:
            width = eps_planes * strip
            pieces = [
                turned[:, comps * strip + k * width : comps * strip + (k + 1) * width].astype(jnp.float32)
                for k in range(2)
            ]
            joined = pieces[0] + pieces[1]
            inverse_cols = joined.T.reshape(eps_planes, strip, line_cells)
            turned = turned[:, : comps * strip]
        solved = solve_turned(turned, inverse_held if instant == 0 else inverse)
        solved = solved.reshape(6, planes, strip, line_cells)
        fields = tuple(solved[i] for i in range(6))
        snapshot = fwd_e[instant].astype(jnp.float32)
        intersection = fields[0] * snapshot[0] + fields[1] * snapshot[1] + fields[2] * snapshot[2]
        gradient = gradient + mask_weight * intersection * (inverse_cols * inverse_cols)
    out = jnp.stack(fields)
    return (out[:3], out[3:], gradient)


def solution(mesh):
    in_specs = (
        P(None, "exc", "line", None),
        P(None, "exc", "line", None),
        P(None, None, "exc", "line", None),
        P(None, "line", None),
        P(None, "line", None),
        P(),
        P("exc"),
        P("exc"),
        P("exc"),
    )
    out_specs = (P(None, "exc", "line", None), P(None, "exc", "line", None), P("exc", "line", None))
    return jax.shard_map(
        per_device, mesh=mesh, in_specs=in_specs, out_specs=out_specs, check_vma=False
    )
```

```python
import jax
import jax.numpy as jnp
from jax import lax
from jax.sharding import PartitionSpec as P

COURANT = 0.4


def line_solve(rounded, inverse):
    flattened = rounded.reshape(-1, rounded.shape[-1])
    solved = lax.dot_general(
        flattened, inverse, (((1,), (1,)), ((), ())), preferred_element_type=jnp.float32
    )
    return solved.reshape(rounded.shape)


def turn_rows(block, line_count):
    comps, strip, cells = block.shape
    parts = block.reshape(comps, strip, line_count, strip)
    parts = jnp.transpose(parts, (2, 1, 0, 3)).reshape(line_count, strip, comps * strip)
    parts = lax.all_to_all(parts, "line", 0, 0, tiled=True)
    return parts.reshape(line_count * strip, comps * strip)


def solve_turned(turned, inverse):
    return lax.dot_general(
        turned, inverse, (((0,), (1,)), ((), ())), preferred_element_type=jnp.float32
    )


def bf16_parts(values):
    high = lax.reduce_precision(values, exponent_bits=8, mantissa_bits=7)
    return [high, values - high]


def shift_down(f, along, first):
    inner = f.shape[along]
    return jnp.concatenate([first, lax.slice_in_dim(f, 0, inner - 1, axis=along)], axis=along)


def shift_up(f, along, last):
    inner = f.shape[along]
    return jnp.concatenate([lax.slice_in_dim(f, 1, inner, axis=along), last], axis=along)


def zeros_like_slice(f, along):
    shape = list(f.shape)
    shape[along] = 1
    return jnp.zeros(shape, f.dtype)


def curl_y(fields, scaled, along, below=None, above=None):
    ex, ey, ez, hx, hy, hz = fields
    if below is None:
        below = (zeros_like_slice(hx, along), zeros_like_slice(hz, along))
    if above is None:
        z = zeros_like_slice(hx, along)
        above = (z, z, z, z, z)
    hx_prev = shift_down(hx, along, below[0])
    hz_prev = shift_down(hz, along, below[1])
    ex = ex + scaled * (hz - hz_prev)
    ez = ez - scaled * (hx - hx_prev)
    last = lax.slice_in_dim(hx, hx.shape[along] - 1, hx.shape[along], axis=along)
    last_z = lax.slice_in_dim(hz, hz.shape[along] - 1, hz.shape[along], axis=along)
    ex_a, ez_a, hx_a, hz_a, scaled_a = above
    ex_next_edge = ex_a + scaled_a * (hz_a - last_z)
    ez_next_edge = ez_a - scaled_a * (hx_a - last)
    ex_next = shift_up(ex, along, ex_next_edge)
    ez_next = shift_up(ez, along, ez_next_edge)
    hx = hx - COURANT * (ez_next - ez)
    hz = hz + COURANT * (ex_next - ex)
    return (ex, ey, ez, hx, hy, hz)


def curl_xz(fields, scaled, along_x, along_z):
    ex, ey, ez, hx, hy, hz = fields

    def lower(f, along):
        return f - shift_down(f, along, zeros_like_slice(f, along))

    def upper(f, along):
        return shift_up(f, along, zeros_like_slice(f, along)) - f

    ex = ex - scaled * lower(hy, along_z)
    ey = ey + scaled * (lower(hx, along_z) - lower(hz, along_x))
    ez = ez + scaled * lower(hy, along_x)
    hx = hx + COURANT * upper(ey, along_z)
    hy = hy + COURANT * (upper(ez, along_x) - upper(ex, along_z))
    hz = hz - COURANT * upper(ey, along_x)
    return (ex, ey, ez, hx, hy, hz)


def per_device(
    adj_e, adj_h, fwd_e, permittivity, design_mask, inverse, omega, port_mode, port_plane
):
    line_cells = inverse.shape[0]
    strip = adj_e.shape[2]
    planes = adj_e.shape[1]
    eps_planes = permittivity.shape[0]
    step_count = fwd_e.shape[0]
    line_count = lax.axis_size("line")
    index = lax.axis_index("line")
    offset = index * strip
    inverse_rows = 1.0 / permittivity
    scaled_rows = COURANT * inverse_rows
    frequency = omega[0]
    plane_at = port_plane[0]
    mask_weight = design_mask.astype(jnp.float32)
    gradient = jnp.zeros(design_mask.shape, jnp.float32)
    comps = 6 * planes

    column = (jnp.arange(line_cells, dtype=jnp.int32) == plane_at).astype(jnp.float32)
    profile_rows = lax.dynamic_slice_in_dim(port_mode, offset, strip)
    amplitude = jnp.cos(frequency * 1.0)
    ex, ey, ez = adj_e[0], adj_e[1], adj_e[2]
    hx, hy, hz = adj_h[0], adj_h[1], adj_h[2]
    ez = ez + (amplitude * profile_rows[None, :, None]) * column[None, None, :]
    is_first = index == 0
    ring = [(i, (i + 1) % line_count) for i in range(line_count)]
    scaled_planes = jnp.broadcast_to(scaled_rows, ex.shape)
    message = jnp.stack(
        [f[:, -1:] for f in (ex, ey, ez, hx, hy, hz, scaled_planes)] + [hx[:, -2:-1], hz[:, -2:-1]]
    )
    message = lax.ppermute(message, "line", ring)
    p_ex, p_ey, p_ez, p_hx, p_hy, p_hz, p_r, p_hx2, p_hz2 = (message[i] for i in range(9))
    zero_row = jnp.zeros_like(p_hx)
    hx_prev = shift_down(hx, 1, jnp.where(is_first, zero_row, p_hx))
    hz_prev = shift_down(hz, 1, jnp.where(is_first, zero_row, p_hz))
    ex1 = ex + scaled_rows * (hz - hz_prev)
    ez1 = ez - scaled_rows * (hx - hx_prev)
    hx1 = hx[:, :-1] - COURANT * (ez1[:, 1:] - ez1[:, :-1])
    hz1 = hz[:, :-1] + COURANT * (ex1[:, 1:] - ex1[:, :-1])
    ex_y = p_ex + p_r * (p_hz - p_hz2)
    ez_y = p_ez - p_r * (p_hx - p_hx2)
    ex_next = jnp.where(is_first, zero_row, ex1[:, :1])
    ez_next = jnp.where(is_first, zero_row, ez1[:, :1])
    hx_y = p_hx - COURANT * (ez_next - ez_y)
    hz_y = p_hz + COURANT * (ex_next - ex_y)
    fields = (
        jnp.concatenate([ex_y, ex1[:, :-1]], 1),
        jnp.concatenate([p_ey, ey[:, :-1]], 1),
        jnp.concatenate([ez_y, ez1[:, :-1]], 1),
        jnp.concatenate([hx_y, hx1], 1),
        jnp.concatenate([p_hy, hy[:, :-1]], 1),
        jnp.concatenate([hz_y, hz1], 1),
    )
    scaled_held = jnp.concatenate([p_r[:eps_planes], scaled_rows[:, :-1]], 1)
    inverse_held = jnp.roll(inverse, 1, axis=1)
    inverse_cols = None
    intersections = []
    for instant in range(step_count):
        if instant > 0:
            amplitude = jnp.cos(frequency * (instant + 1))
            x_local = offset + jnp.arange(strip, dtype=jnp.int32)
            column_local = (x_local == plane_at).astype(jnp.float32)
            ex, ey, ez, hx, hy, hz = fields
            ez = ez + (amplitude * column_local[None, :, None]) * port_mode[None, None, :]
            fields = curl_y((ex, ey, ez, hx, hy, hz), COURANT * inverse_cols, 2)
            rounded = jnp.stack(fields).reshape(comps, strip, line_cells).astype(jnp.bfloat16)
            solved = solve_turned(turn_rows(rounded, line_count), inverse)
        else:
            rounded = jnp.stack(fields).astype(jnp.bfloat16)
            solved = line_solve(rounded, inverse)
        solved = solved.reshape(6, planes, strip, line_cells)
        fields = curl_xz(
            tuple(solved[i] for i in range(6)), scaled_held if instant == 0 else scaled_rows, 2, 0
        )
        stacked = jnp.stack(fields).reshape(comps, strip, line_cells)
        if inverse_cols is None:
            stacked = jnp.concatenate([stacked] + bf16_parts(inverse_rows), 0)
        turned = turn_rows(stacked.astype(jnp.bfloat16), line_count)
        if inverse_cols is None:
            width = eps_planes * strip
            pieces = [
                turned[:, comps * strip + k * width : comps * strip + (k + 1) * width].astype(jnp.float32)
                for k in range(2)
            ]
            joined = pieces[0] + pieces[1]
            inverse_cols = joined.T.reshape(eps_planes, strip, line_cells)
            turned = turned[:, : comps * strip]
        solved = solve_turned(turned, inverse_held if instant == 0 else inverse)
        solved = solved.reshape(6, planes, strip, line_cells)
        fields = tuple(solved[i] for i in range(6))
        intersections.append((instant, fields[:3]))
    for instant, electric in intersections:
        snapshot = fwd_e[instant].astype(jnp.float32)
        intersection = electric[0] * snapshot[0] + electric[1] * snapshot[1] + electric[2] * snapshot[2]
        gradient = gradient + mask_weight * intersection * (inverse_cols * inverse_cols)
    out = jnp.stack(fields)
    return (out[:3], out[3:], gradient)


def solution(mesh):
    in_specs = (
        P(None, "exc", "line", None),
        P(None, "exc", "line", None),
        P(None, None, "exc", "line", None),
        P(None, "line", None),
        P(None, "line", None),
        P(),
        P("exc"),
        P("exc"),
        P("exc"),
    )
    out_specs = (P(None, "exc", "line", None), P(None, "exc", "line", None), P("exc", "line", None))
    return jax.shard_map(
        per_device, mesh=mesh, in_specs=in_specs, out_specs=out_specs, check_vma=False
    )
```

```python
import jax
import jax.numpy as jnp
from jax import lax
from jax.sharding import PartitionSpec as P

COURANT = 0.4


def line_solve(rounded, inverse):
    flattened = rounded.reshape(-1, rounded.shape[-1])
    solved = lax.dot_general(
        flattened, inverse, (((1,), (1,)), ((), ())), preferred_element_type=jnp.float32
    )
    return solved.reshape(rounded.shape)


def turn_rows(block, line_count):
    comps, strip, cells = block.shape
    parts = block.reshape(comps, strip, line_count, strip)
    parts = jnp.transpose(parts, (2, 1, 0, 3)).reshape(line_count, strip, comps * strip)
    parts = lax.all_to_all(parts, "line", 0, 0, tiled=True)
    return parts.reshape(line_count * strip, comps * strip)


def solve_turned(turned, inverse):
    return lax.dot_general(
        turned, inverse, (((0,), (1,)), ((), ())), preferred_element_type=jnp.float32
    )


def bf16_parts(values):
    high = lax.reduce_precision(values, exponent_bits=8, mantissa_bits=7)
    return [high, values - high]


def shift_down(f, along, first):
    inner = f.shape[along]
    return jnp.concatenate([first, lax.slice_in_dim(f, 0, inner - 1, axis=along)], axis=along)


def shift_up(f, along, last):
    inner = f.shape[along]
    return jnp.concatenate([lax.slice_in_dim(f, 1, inner, axis=along), last], axis=along)


def zeros_like_slice(f, along):
    shape = list(f.shape)
    shape[along] = 1
    return jnp.zeros(shape, f.dtype)


def curl_y(fields, scaled, along, below=None, above=None):
    ex, ey, ez, hx, hy, hz = fields
    if below is None:
        below = (zeros_like_slice(hx, along), zeros_like_slice(hz, along))
    if above is None:
        z = zeros_like_slice(hx, along)
        above = (z, z, z, z, z)
    hx_prev = shift_down(hx, along, below[0])
    hz_prev = shift_down(hz, along, below[1])
    ex = ex + scaled * (hz - hz_prev)
    ez = ez - scaled * (hx - hx_prev)
    last = lax.slice_in_dim(hx, hx.shape[along] - 1, hx.shape[along], axis=along)
    last_z = lax.slice_in_dim(hz, hz.shape[along] - 1, hz.shape[along], axis=along)
    ex_a, ez_a, hx_a, hz_a, scaled_a = above
    ex_next_edge = ex_a + scaled_a * (hz_a - last_z)
    ez_next_edge = ez_a - scaled_a * (hx_a - last)
    ex_next = shift_up(ex, along, ex_next_edge)
    ez_next = shift_up(ez, along, ez_next_edge)
    hx = hx - COURANT * (ez_next - ez)
    hz = hz + COURANT * (ex_next - ex)
    return (ex, ey, ez, hx, hy, hz)


def curl_xz(fields, scaled, along_x, along_z):
    ex, ey, ez, hx, hy, hz = fields

    def lower(f, along):
        return f - shift_down(f, along, zeros_like_slice(f, along))

    def upper(f, along):
        return shift_up(f, along, zeros_like_slice(f, along)) - f

    ex = ex - scaled * lower(hy, along_z)
    ey = ey + scaled * (lower(hx, along_z) - lower(hz, along_x))
    ez = ez + scaled * lower(hy, along_x)
    hx = hx + COURANT * upper(ey, along_z)
    hy = hy + COURANT * (upper(ez, along_x) - upper(ex, along_z))
    hz = hz - COURANT * upper(ey, along_x)
    return (ex, ey, ez, hx, hy, hz)


def per_device(
    adj_e, adj_h, fwd_e, permittivity, design_mask, inverse, omega, port_mode, port_plane
):
    line_cells = inverse.shape[0]
    strip = adj_e.shape[2]
    planes = adj_e.shape[1]
    eps_planes = permittivity.shape[0]
    step_count = fwd_e.shape[0]
    line_count = lax.axis_size("line")
    index = lax.axis_index("line")
    offset = index * strip
    inverse_rows = 1.0 / permittivity
    scaled_rows = COURANT * inverse_rows
    frequency = omega[0]
    plane_at = port_plane[0]
    mask_weight = design_mask.astype(jnp.float32)
    gradient = jnp.zeros(design_mask.shape, jnp.float32)
    comps = 6 * planes

    column = (jnp.arange(line_cells, dtype=jnp.int32) == plane_at).astype(jnp.float32)
    profile_rows = lax.dynamic_slice_in_dim(port_mode, offset, strip)
    amplitude = jnp.cos(frequency * 1.0)
    ex, ey, ez = adj_e[0], adj_e[1], adj_e[2]
    hx, hy, hz = adj_h[0], adj_h[1], adj_h[2]
    ez = ez + (amplitude * profile_rows[None, :, None]) * column[None, None, :]
    up = [(i, i + 1) for i in range(line_count - 1)]
    scaled_planes = jnp.broadcast_to(scaled_rows, ex.shape)
    message = jnp.stack(
        [f[:, -1:] for f in (ex, ey, ez, hx, hy, hz, scaled_planes)] + [hx[:, -2:-1], hz[:, -2:-1]]
    )
    message = lax.ppermute(message, "line", up)
    p_ex, p_ey, p_ez, p_hx, p_hy, p_hz, p_r, p_hx2, p_hz2 = (message[i] for i in range(9))
    hx_prev = shift_down(hx, 1, p_hx)
    hz_prev = shift_down(hz, 1, p_hz)
    ex1 = ex + scaled_rows * (hz - hz_prev)
    ez1 = ez - scaled_rows * (hx - hx_prev)
    hx1 = hx[:, :-1] - COURANT * (ez1[:, 1:] - ez1[:, :-1])
    hz1 = hz[:, :-1] + COURANT * (ex1[:, 1:] - ex1[:, :-1])
    hx_last = hx[:, -1:] - COURANT * (0.0 - ez1[:, -1:])
    hz_last = hz[:, -1:] + COURANT * (0.0 - ex1[:, -1:])
    ex_y = p_ex + p_r * (p_hz - p_hz2)
    ez_y = p_ez - p_r * (p_hx - p_hx2)
    hx_y = p_hx - COURANT * (ez1[:, :1] - ez_y)
    hz_y = p_hz + COURANT * (ex1[:, :1] - ex_y)
    fields = (
        jnp.concatenate([ex_y, ex1], 1),
        jnp.concatenate([p_ey, ey], 1),
        jnp.concatenate([ez_y, ez1], 1),
        jnp.concatenate([hx_y, hx1, hx_last], 1),
        jnp.concatenate([p_hy, hy], 1),
        jnp.concatenate([hz_y, hz1, hz_last], 1),
    )
    scaled_held = jnp.concatenate([p_r[:eps_planes], scaled_rows], 1)
    inverse_held = jnp.roll(inverse, 1, axis=1)
    inverse_cols = None
    for instant in range(step_count):
        if instant > 0:
            amplitude = jnp.cos(frequency * (instant + 1))
            x_local = offset + jnp.arange(strip, dtype=jnp.int32)
            column_local = (x_local == plane_at).astype(jnp.float32)
            ex, ey, ez, hx, hy, hz = fields
            ez = ez + (amplitude * column_local[None, :, None]) * port_mode[None, None, :]
            fields = curl_y((ex, ey, ez, hx, hy, hz), COURANT * inverse_cols, 2)
            rounded = jnp.stack(fields).reshape(comps, strip, line_cells).astype(jnp.bfloat16)
            solved = solve_turned(turn_rows(rounded, line_count), inverse)
        else:
            rounded = jnp.stack(fields).astype(jnp.bfloat16)
            solved = line_solve(rounded, inverse)
        solved = solved.reshape(6, planes, -1, line_cells)
        fields = curl_xz(
            tuple(solved[i] for i in range(6)), scaled_held if instant == 0 else scaled_rows, 2, 0
        )
        if inverse_cols is None:
            stacked = jnp.stack(fields).reshape(comps, strip + 1, line_cells)
            spare = jnp.zeros((eps_planes, 1, line_cells), jnp.float32)
            eps_parts = [jnp.concatenate([p, spare], 1) for p in bf16_parts(inverse_rows)]
            stacked = jnp.concatenate([stacked] + eps_parts, 0).astype(jnp.bfloat16)
            slots = stacked.shape[0]
            parts = stacked.reshape(slots, strip + 1, line_count, strip)
            parts = jnp.transpose(parts, (2, 1, 0, 3)).reshape(line_count, strip + 1, slots * strip)
            parts = lax.all_to_all(parts, "line", 0, 0, tiled=True)
            held = parts[:, :strip].at[0, 0, : comps * strip].set(parts[line_count - 1, strip, : comps * strip])
            turned = held.reshape(line_count * strip, slots * strip)
        else:
            stacked = jnp.stack(fields).reshape(comps, strip, line_cells)
            turned = turn_rows(stacked.astype(jnp.bfloat16), line_count)
        if inverse_cols is None:
            width = eps_planes * strip
            pieces = [
                turned[:, comps * strip + k * width : comps * strip + (k + 1) * width].astype(jnp.float32)
                for k in range(2)
            ]
            joined = pieces[0] + pieces[1]
            inverse_cols = joined.T.reshape(eps_planes, strip, line_cells)
            turned = turned[:, : comps * strip]
        solved = solve_turned(turned, inverse_held if instant == 0 else inverse)
        solved = solved.reshape(6, planes, strip, line_cells)
        fields = tuple(solved[i] for i in range(6))
        snapshot = fwd_e[instant].astype(jnp.float32)
        intersection = fields[0] * snapshot[0] + fields[1] * snapshot[1] + fields[2] * snapshot[2]
        gradient = gradient + mask_weight * intersection * (inverse_cols * inverse_cols)
    out = jnp.stack(fields)
    return (out[:3], out[3:], gradient)


def solution(mesh):
    in_specs = (
        P(None, "exc", "line", None),
        P(None, "exc", "line", None),
        P(None, None, "exc", "line", None),
        P(None, "line", None),
        P(None, "line", None),
        P(),
        P("exc"),
        P("exc"),
        P("exc"),
    )
    out_specs = (P(None, "exc", "line", None), P(None, "exc", "line", None), P("exc", "line", None))
    return jax.shard_map(
        per_device, mesh=mesh, in_specs=in_specs, out_specs=out_specs, check_vma=False
    )
```

```python
import jax
import jax.numpy as jnp
from jax import lax
from jax.sharding import PartitionSpec as P

COURANT = 0.4


def line_solve(rounded, inverse):
    flattened = rounded.reshape(-1, rounded.shape[-1])
    solved = lax.dot_general(
        flattened, inverse, (((1,), (1,)), ((), ())), preferred_element_type=jnp.float32
    )
    return solved.reshape(rounded.shape)


def turn_rows(block, line_count):
    comps, strip, cells = block.shape
    parts = block.reshape(comps, strip, line_count, strip)
    parts = jnp.transpose(parts, (2, 1, 0, 3)).reshape(line_count, strip, comps * strip)
    parts = lax.all_to_all(parts, "line", 0, 0, tiled=True)
    return parts.reshape(line_count * strip, comps * strip)


def solve_turned(turned, inverse):
    return lax.dot_general(
        turned, inverse, (((0,), (1,)), ((), ())), preferred_element_type=jnp.float32
    )


def bf16_parts(values):
    high = lax.reduce_precision(values, exponent_bits=8, mantissa_bits=7)
    return [high, values - high]


def shift_down(f, along, first):
    inner = f.shape[along]
    return jnp.concatenate([first, lax.slice_in_dim(f, 0, inner - 1, axis=along)], axis=along)


def shift_up(f, along, last):
    inner = f.shape[along]
    return jnp.concatenate([lax.slice_in_dim(f, 1, inner, axis=along), last], axis=along)


def zeros_like_slice(f, along):
    shape = list(f.shape)
    shape[along] = 1
    return jnp.zeros(shape, f.dtype)


def curl_y(fields, scaled, along, below=None, above=None):
    ex, ey, ez, hx, hy, hz = fields
    if below is None:
        below = (zeros_like_slice(hx, along), zeros_like_slice(hz, along))
    if above is None:
        z = zeros_like_slice(hx, along)
        above = (z, z, z, z, z)
    hx_prev = shift_down(hx, along, below[0])
    hz_prev = shift_down(hz, along, below[1])
    ex = ex + scaled * (hz - hz_prev)
    ez = ez - scaled * (hx - hx_prev)
    last = lax.slice_in_dim(hx, hx.shape[along] - 1, hx.shape[along], axis=along)
    last_z = lax.slice_in_dim(hz, hz.shape[along] - 1, hz.shape[along], axis=along)
    ex_a, ez_a, hx_a, hz_a, scaled_a = above
    ex_next_edge = ex_a + scaled_a * (hz_a - last_z)
    ez_next_edge = ez_a - scaled_a * (hx_a - last)
    ex_next = shift_up(ex, along, ex_next_edge)
    ez_next = shift_up(ez, along, ez_next_edge)
    hx = hx - COURANT * (ez_next - ez)
    hz = hz + COURANT * (ex_next - ex)
    return (ex, ey, ez, hx, hy, hz)


def curl_xz(fields, scaled, along_x, along_z):
    ex, ey, ez, hx, hy, hz = fields

    def lower(f, along):
        return f - shift_down(f, along, zeros_like_slice(f, along))

    def upper(f, along):
        return shift_up(f, along, zeros_like_slice(f, along)) - f

    ex = ex - scaled * lower(hy, along_z)
    ey = ey + scaled * (lower(hx, along_z) - lower(hz, along_x))
    ez = ez + scaled * lower(hy, along_x)
    hx = hx + COURANT * upper(ey, along_z)
    hy = hy + COURANT * (upper(ez, along_x) - upper(ex, along_z))
    hz = hz - COURANT * upper(ey, along_x)
    return (ex, ey, ez, hx, hy, hz)


def per_device(
    adj_e, adj_h, fwd_e, permittivity, design_mask, inverse, omega, port_mode, port_plane
):
    line_cells = inverse.shape[0]
    strip = adj_e.shape[2]
    planes = adj_e.shape[1]
    eps_planes = permittivity.shape[0]
    step_count = fwd_e.shape[0]
    line_count = lax.axis_size("line")
    index = lax.axis_index("line")
    offset = index * strip
    inverse_rows = 1.0 / permittivity
    scaled_rows = COURANT * inverse_rows
    frequency = omega[0]
    plane_at = port_plane[0]
    mask_weight = design_mask.astype(jnp.float32)
    gradient = jnp.zeros(design_mask.shape, jnp.float32)
    comps = 6 * planes

    column = (jnp.arange(line_cells, dtype=jnp.int32) == plane_at).astype(jnp.float32)
    profile_rows = lax.dynamic_slice_in_dim(port_mode, offset, strip)
    amplitude = jnp.cos(frequency * 1.0)
    ex, ey, ez = adj_e[0], adj_e[1], adj_e[2]
    hx, hy, hz = adj_h[0], adj_h[1], adj_h[2]
    ez = ez + (amplitude * profile_rows[None, :, None]) * column[None, None, :]
    is_first = index == 0
    ring = [(i, (i + 1) % line_count) for i in range(line_count)]
    eps_planes_b = jnp.broadcast_to(permittivity, ex.shape)
    message = jnp.stack(
        [f[:, -1:] for f in (ex, ey, ez, hx, hy, hz, eps_planes_b)] + [hx[:, -2:-1], hz[:, -2:-1]]
    )
    message = lax.ppermute(message, "line", ring)
    p_ex, p_ey, p_ez, p_hx, p_hy, p_hz, p_eps, p_hx2, p_hz2 = (message[i] for i in range(9))
    p_r = COURANT * (1.0 / p_eps)
    zero_row = jnp.zeros_like(p_hx)
    hx_prev = shift_down(hx, 1, jnp.where(is_first, zero_row, p_hx))
    hz_prev = shift_down(hz, 1, jnp.where(is_first, zero_row, p_hz))
    ex1 = ex + scaled_rows * (hz - hz_prev)
    ez1 = ez - scaled_rows * (hx - hx_prev)
    hx1 = hx[:, :-1] - COURANT * (ez1[:, 1:] - ez1[:, :-1])
    hz1 = hz[:, :-1] + COURANT * (ex1[:, 1:] - ex1[:, :-1])
    ex_y = p_ex + p_r * (p_hz - p_hz2)
    ez_y = p_ez - p_r * (p_hx - p_hx2)
    ex_next = jnp.where(is_first, zero_row, ex1[:, :1])
    ez_next = jnp.where(is_first, zero_row, ez1[:, :1])
    hx_y = p_hx - COURANT * (ez_next - ez_y)
    hz_y = p_hz + COURANT * (ex_next - ex_y)
    fields = (
        jnp.concatenate([ex_y, ex1[:, :-1]], 1),
        jnp.concatenate([p_ey, ey[:, :-1]], 1),
        jnp.concatenate([ez_y, ez1[:, :-1]], 1),
        jnp.concatenate([hx_y, hx1], 1),
        jnp.concatenate([p_hy, hy[:, :-1]], 1),
        jnp.concatenate([hz_y, hz1], 1),
    )
    scaled_held = jnp.concatenate([p_r[:eps_planes], scaled_rows[:, :-1]], 1)
    inverse_held = jnp.roll(inverse, 1, axis=1)
    inverse_cols = None
    for instant in range(step_count):
        if instant > 0:
            amplitude = jnp.cos(frequency * (instant + 1))
            x_local = offset + jnp.arange(strip, dtype=jnp.int32)
            column_local = (x_local == plane_at).astype(jnp.float32)
            ex, ey, ez, hx, hy, hz = fields
            ez = ez + (amplitude * column_local[None, :, None]) * port_mode[None, None, :]
            fields = curl_y((ex, ey, ez, hx, hy, hz), COURANT * inverse_cols, 2)
            rounded = jnp.stack(fields).reshape(comps, strip, line_cells).astype(jnp.bfloat16)
            solved = solve_turned(turn_rows(rounded, line_count), inverse)
        else:
            rounded = jnp.stack(fields).astype(jnp.bfloat16)
            solved = line_solve(rounded, inverse)
        solved = solved.reshape(6, planes, strip, line_cells)
        fields = curl_xz(
            tuple(solved[i] for i in range(6)), scaled_held if instant == 0 else scaled_rows, 2, 0
        )
        stacked = jnp.stack(fields).reshape(comps, strip, line_cells)
        if inverse_cols is None:
            stacked = jnp.concatenate([stacked] + bf16_parts(inverse_rows), 0)
        turned = turn_rows(stacked.astype(jnp.bfloat16), line_count)
        if inverse_cols is None:
            width = eps_planes * strip
            pieces = [
                turned[:, comps * strip + k * width : comps * strip + (k + 1) * width].astype(jnp.float32)
                for k in range(2)
            ]
            joined = pieces[0] + pieces[1]
            inverse_cols = joined.T.reshape(eps_planes, strip, line_cells)
            turned = turned[:, : comps * strip]
        solved = solve_turned(turned, inverse_held if instant == 0 else inverse)
        solved = solved.reshape(6, planes, strip, line_cells)
        fields = tuple(solved[i] for i in range(6))
        snapshot = fwd_e[instant].astype(jnp.float32)
        intersection = fields[0] * snapshot[0] + fields[1] * snapshot[1] + fields[2] * snapshot[2]
        gradient = gradient + mask_weight * intersection * (inverse_cols * inverse_cols)
    out = jnp.stack(fields)
    return (out[:3], out[3:], gradient)


def solution(mesh):
    in_specs = (
        P(None, "exc", "line", None),
        P(None, "exc", "line", None),
        P(None, None, "exc", "line", None),
        P(None, "line", None),
        P(None, "line", None),
        P(),
        P("exc"),
        P("exc"),
        P("exc"),
    )
    out_specs = (P(None, "exc", "line", None), P(None, "exc", "line", None), P("exc", "line", None))
    return jax.shard_map(
        per_device, mesh=mesh, in_specs=in_specs, out_specs=out_specs, check_vma=False
    )
```

```python
import jax
import jax.numpy as jnp
from jax import lax
from jax.sharding import PartitionSpec as P

COURANT = 0.4


def line_solve(rounded, inverse):
    flattened = rounded.reshape(-1, rounded.shape[-1])
    solved = lax.dot_general(
        flattened, inverse, (((1,), (1,)), ((), ())), preferred_element_type=jnp.float32
    )
    return solved.reshape(rounded.shape)


def turn_rows(block, line_count):
    comps, strip, cells = block.shape
    parts = block.reshape(comps, strip, line_count, strip)
    parts = jnp.transpose(parts, (2, 1, 0, 3)).reshape(line_count, strip, comps * strip)
    parts = lax.all_to_all(parts, "line", 0, 0, tiled=True)
    return parts.reshape(line_count * strip, comps * strip)


def solve_turned(turned, inverse):
    return lax.dot_general(
        turned, inverse, (((0,), (1,)), ((), ())), preferred_element_type=jnp.float32
    )


def bf16_parts(values):
    high = lax.reduce_precision(values, exponent_bits=8, mantissa_bits=7)
    return [high, values - high]


def shift_down(f, along, first):
    inner = f.shape[along]
    return jnp.concatenate([first, lax.slice_in_dim(f, 0, inner - 1, axis=along)], axis=along)


def shift_up(f, along, last):
    inner = f.shape[along]
    return jnp.concatenate([lax.slice_in_dim(f, 1, inner, axis=along), last], axis=along)


def zeros_like_slice(f, along):
    shape = list(f.shape)
    shape[along] = 1
    return jnp.zeros(shape, f.dtype)


def curl_y(fields, scaled, along, below=None, above=None):
    ex, ey, ez, hx, hy, hz = fields
    if below is None:
        below = (zeros_like_slice(hx, along), zeros_like_slice(hz, along))
    if above is None:
        z = zeros_like_slice(hx, along)
        above = (z, z, z, z, z)
    hx_prev = shift_down(hx, along, below[0])
    hz_prev = shift_down(hz, along, below[1])
    ex = ex + scaled * (hz - hz_prev)
    ez = ez - scaled * (hx - hx_prev)
    last = lax.slice_in_dim(hx, hx.shape[along] - 1, hx.shape[along], axis=along)
    last_z = lax.slice_in_dim(hz, hz.shape[along] - 1, hz.shape[along], axis=along)
    ex_a, ez_a, hx_a, hz_a, scaled_a = above
    ex_next_edge = ex_a + scaled_a * (hz_a - last_z)
    ez_next_edge = ez_a - scaled_a * (hx_a - last)
    ex_next = shift_up(ex, along, ex_next_edge)
    ez_next = shift_up(ez, along, ez_next_edge)
    hx = hx - COURANT * (ez_next - ez)
    hz = hz + COURANT * (ex_next - ex)
    return (ex, ey, ez, hx, hy, hz)


def curl_xz(fields, scaled, along_x, along_z):
    ex, ey, ez, hx, hy, hz = fields

    def lower(f, along):
        return f - shift_down(f, along, zeros_like_slice(f, along))

    def upper(f, along):
        return shift_up(f, along, zeros_like_slice(f, along)) - f

    ex = ex - scaled * lower(hy, along_z)
    ey = ey + scaled * (lower(hx, along_z) - lower(hz, along_x))
    ez = ez + scaled * lower(hy, along_x)
    hx = hx + COURANT * upper(ey, along_z)
    hy = hy + COURANT * (upper(ez, along_x) - upper(ex, along_z))
    hz = hz - COURANT * upper(ey, along_x)
    return (ex, ey, ez, hx, hy, hz)


def per_device(
    adj_e, adj_h, fwd_e, permittivity, design_mask, inverse, omega, port_mode, port_plane
):
    line_cells = inverse.shape[0]
    strip = adj_e.shape[2]
    planes = adj_e.shape[1]
    eps_planes = permittivity.shape[0]
    step_count = fwd_e.shape[0]
    line_count = lax.axis_size("line")
    index = lax.axis_index("line")
    offset = index * strip
    inverse_rows = 1.0 / permittivity
    scaled_rows = COURANT * inverse_rows
    frequency = omega[0]
    plane_at = port_plane[0]
    mask_weight = design_mask.astype(jnp.float32)
    gradient = jnp.zeros(design_mask.shape, jnp.float32)
    comps = 6 * planes

    ring = [(i, (i + 1) % line_count) for i in range(line_count)]
    is_first = index == 0
    column = (jnp.arange(line_cells, dtype=jnp.int32) == plane_at).astype(jnp.float32)
    profile_rows = lax.dynamic_slice_in_dim(port_mode, offset, strip)
    amplitude = jnp.cos(frequency * 1.0)
    ex, ey, ez = adj_e[0], adj_e[1], adj_e[2]
    hx, hy, hz = adj_h[0], adj_h[1], adj_h[2]
    ez = ez + (amplitude * profile_rows[None, :, None]) * column[None, None, :]
    scaled_planes = jnp.broadcast_to(scaled_rows, ex.shape)
    message = jnp.stack(
        [f[:, -1:] for f in (ex, ey, ez, hx, hy, hz, scaled_planes)] + [hx[:, -2:-1], hz[:, -2:-1]]
    )
    message = lax.ppermute(message, "line", ring)
    ex1 = ex[:, 1:] + scaled_rows[:, 1:] * (hz[:, 1:] - hz[:, :-1])
    ez1 = ez[:, 1:] - scaled_rows[:, 1:] * (hx[:, 1:] - hx[:, :-1])
    hx1 = hx[:, 1:-1] - COURANT * (ez1[:, 1:] - ez1[:, :-1])
    hz1 = hz[:, 1:-1] + COURANT * (ex1[:, 1:] - ex1[:, :-1])
    inner = (ex1[:, :-1], ey[:, 1:-1], ez1[:, :-1], hx1, hy[:, 1:-1], hz1)
    inner_solved = line_solve(jnp.stack(inner).astype(jnp.bfloat16), inverse)
    inner_fields = curl_xz(tuple(inner_solved[i] for i in range(6)), scaled_rows[:, 1:-1], 2, 0)
    p_ex, p_ey, p_ez, p_hx, p_hy, p_hz, p_r, p_hx2, p_hz2 = (message[i] for i in range(9))
    zero_row = jnp.zeros_like(p_hx)
    below_hx = jnp.where(is_first, zero_row, p_hx)
    below_hz = jnp.where(is_first, zero_row, p_hz)
    ex_0 = ex[:, :1] + scaled_rows[:, :1] * (hz[:, :1] - below_hz)
    ez_0 = ez[:, :1] - scaled_rows[:, :1] * (hx[:, :1] - below_hx)
    hx_0 = hx[:, :1] - COURANT * (ez1[:, :1] - ez_0)
    hz_0 = hz[:, :1] + COURANT * (ex1[:, :1] - ex_0)
    ex_y = p_ex + p_r * (p_hz - p_hz2)
    ez_y = p_ez - p_r * (p_hx - p_hx2)
    ex_next = jnp.where(is_first, zero_row, ex_0)
    ez_next = jnp.where(is_first, zero_row, ez_0)
    hx_y = p_hx - COURANT * (ez_next - ez_y)
    hz_y = p_hz + COURANT * (ex_next - ex_y)
    edge = (
        jnp.concatenate([ex_y, ex_0], 1),
        jnp.concatenate([p_ey, ey[:, :1]], 1),
        jnp.concatenate([ez_y, ez_0], 1),
        jnp.concatenate([hx_y, hx_0], 1),
        jnp.concatenate([p_hy, hy[:, :1]], 1),
        jnp.concatenate([hz_y, hz_0], 1),
    )
    edge_solved = line_solve(jnp.stack(edge).astype(jnp.bfloat16), inverse)
    scaled_edge = jnp.concatenate([p_r[:eps_planes], scaled_rows[:, :1]], 1)
    edge_fields = curl_xz(tuple(edge_solved[i] for i in range(6)), scaled_edge, 2, 0)
    first_fields = tuple(jnp.concatenate([a, b], 1) for a, b in zip(edge_fields, inner_fields))
    inverse_held = jnp.roll(inverse, 1, axis=1)
    inverse_cols = None
    for instant in range(step_count):
        if instant > 0:
            amplitude = jnp.cos(frequency * (instant + 1))
            x_local = offset + jnp.arange(strip, dtype=jnp.int32)
            column_local = (x_local == plane_at).astype(jnp.float32)
            ex, ey, ez, hx, hy, hz = fields
            ez = ez + (amplitude * column_local[None, :, None]) * port_mode[None, None, :]
            fields = curl_y((ex, ey, ez, hx, hy, hz), COURANT * inverse_cols, 2)
            rounded = jnp.stack(fields).reshape(comps, strip, line_cells).astype(jnp.bfloat16)
            solved = solve_turned(turn_rows(rounded, line_count), inverse)
            solved = solved.reshape(6, planes, strip, line_cells)
            fields = curl_xz(tuple(solved[i] for i in range(6)), scaled_rows, 2, 0)
        else:
            fields = first_fields
        stacked = jnp.stack(fields).reshape(comps, strip, line_cells)
        if inverse_cols is None:
            stacked = jnp.concatenate([stacked] + bf16_parts(inverse_rows), 0)
        turned = turn_rows(stacked.astype(jnp.bfloat16), line_count)
        if inverse_cols is None:
            width = eps_planes * strip
            pieces = [
                turned[:, comps * strip + k * width : comps * strip + (k + 1) * width].astype(jnp.float32)
                for k in range(2)
            ]
            joined = pieces[0] + pieces[1]
            inverse_cols = joined.T.reshape(eps_planes, strip, line_cells)
            turned = turned[:, : comps * strip]
        solved = solve_turned(turned, inverse_held if instant == 0 else inverse)
        solved = solved.reshape(6, planes, strip, line_cells)
        fields = tuple(solved[i] for i in range(6))
        snapshot = fwd_e[instant].astype(jnp.float32)
        intersection = fields[0] * snapshot[0] + fields[1] * snapshot[1] + fields[2] * snapshot[2]
        gradient = gradient + mask_weight * intersection * (inverse_cols * inverse_cols)
    out = jnp.stack(fields)
    return (out[:3], out[3:], gradient)


def solution(mesh):
    in_specs = (
        P(None, "exc", "line", None),
        P(None, "exc", "line", None),
        P(None, None, "exc", "line", None),
        P(None, "line", None),
        P(None, "line", None),
        P(),
        P("exc"),
        P("exc"),
        P("exc"),
    )
    out_specs = (P(None, "exc", "line", None), P(None, "exc", "line", None), P("exc", "line", None))
    return jax.shard_map(
        per_device, mesh=mesh, in_specs=in_specs, out_specs=out_specs, check_vma=False
    )
```

```python
import jax
import jax.numpy as jnp
from jax import lax
from jax.sharding import PartitionSpec as P

COURANT = 0.4


def line_solve(rounded, inverse):
    flattened = rounded.reshape(-1, rounded.shape[-1])
    solved = lax.dot_general(
        flattened, inverse, (((1,), (1,)), ((), ())), preferred_element_type=jnp.float32
    )
    return solved.reshape(rounded.shape)


def turn_rows(block, line_count):
    comps, strip, cells = block.shape
    parts = block.reshape(comps, strip, line_count, strip)
    parts = jnp.transpose(parts, (2, 1, 0, 3)).reshape(line_count, strip, comps * strip)
    parts = lax.all_to_all(parts, "line", 0, 0, tiled=True)
    return parts.reshape(line_count * strip, comps * strip)


def solve_turned(turned, inverse):
    return lax.dot_general(
        turned, inverse, (((0,), (1,)), ((), ())), preferred_element_type=jnp.float32
    )


def bf16_parts(values):
    high = lax.reduce_precision(values, exponent_bits=8, mantissa_bits=7)
    return [high, values - high]


def shift_down(f, along, first):
    inner = f.shape[along]
    return jnp.concatenate([first, lax.slice_in_dim(f, 0, inner - 1, axis=along)], axis=along)


def shift_up(f, along, last):
    inner = f.shape[along]
    return jnp.concatenate([lax.slice_in_dim(f, 1, inner, axis=along), last], axis=along)


def zeros_like_slice(f, along):
    shape = list(f.shape)
    shape[along] = 1
    return jnp.zeros(shape, f.dtype)


def curl_y(fields, scaled, along, below=None, above=None):
    ex, ey, ez, hx, hy, hz = fields
    if below is None:
        below = (zeros_like_slice(hx, along), zeros_like_slice(hz, along))
    if above is None:
        z = zeros_like_slice(hx, along)
        above = (z, z, z, z, z)
    hx_prev = shift_down(hx, along, below[0])
    hz_prev = shift_down(hz, along, below[1])
    ex = ex + scaled * (hz - hz_prev)
    ez = ez - scaled * (hx - hx_prev)
    last = lax.slice_in_dim(hx, hx.shape[along] - 1, hx.shape[along], axis=along)
    last_z = lax.slice_in_dim(hz, hz.shape[along] - 1, hz.shape[along], axis=along)
    ex_a, ez_a, hx_a, hz_a, scaled_a = above
    ex_next_edge = ex_a + scaled_a * (hz_a - last_z)
    ez_next_edge = ez_a - scaled_a * (hx_a - last)
    ex_next = shift_up(ex, along, ex_next_edge)
    ez_next = shift_up(ez, along, ez_next_edge)
    hx = hx - COURANT * (ez_next - ez)
    hz = hz + COURANT * (ex_next - ex)
    return (ex, ey, ez, hx, hy, hz)


def curl_xz(fields, scaled, along_x, along_z):
    ex, ey, ez, hx, hy, hz = fields

    def lower(f, along):
        return f - shift_down(f, along, zeros_like_slice(f, along))

    def upper(f, along):
        return shift_up(f, along, zeros_like_slice(f, along)) - f

    ex = ex - scaled * lower(hy, along_z)
    ey = ey + scaled * (lower(hx, along_z) - lower(hz, along_x))
    ez = ez + scaled * lower(hy, along_x)
    hx = hx + COURANT * upper(ey, along_z)
    hy = hy + COURANT * (upper(ez, along_x) - upper(ex, along_z))
    hz = hz - COURANT * upper(ey, along_x)
    return (ex, ey, ez, hx, hy, hz)


def per_device(
    adj_e, adj_h, fwd_e, permittivity, design_mask, inverse, omega, port_mode, port_plane
):
    line_cells = inverse.shape[0]
    strip = adj_e.shape[2]
    planes = adj_e.shape[1]
    eps_planes = permittivity.shape[0]
    step_count = fwd_e.shape[0]
    line_count = lax.axis_size("line")
    index = lax.axis_index("line")
    offset = index * strip
    inverse_rows = 1.0 / permittivity
    scaled_rows = COURANT * inverse_rows
    frequency = omega[0]
    plane_at = port_plane[0]
    mask_weight = design_mask.astype(jnp.float32)
    gradient = jnp.zeros(design_mask.shape, jnp.float32)
    comps = 6 * planes

    column = (jnp.arange(line_cells, dtype=jnp.int32) == plane_at).astype(jnp.float32)
    profile_rows = lax.dynamic_slice_in_dim(port_mode, offset, strip)
    amplitude = jnp.cos(frequency * 1.0)
    ex, ey, ez = adj_e[0], adj_e[1], adj_e[2]
    hx, hy, hz = adj_h[0], adj_h[1], adj_h[2]
    ez = ez + (amplitude * profile_rows[None, :, None]) * column[None, None, :]
    is_first = index == 0
    ring = [(i, (i + 1) % line_count) for i in range(line_count)]
    scaled_planes = jnp.broadcast_to(scaled_rows, ex.shape)
    message = jnp.stack(
        [f[:, -1:] for f in (ex, ey, ez, hx, hy, hz, scaled_planes)] + [hx[:, -2:-1], hz[:, -2:-1]]
    )
    message = lax.ppermute(message, "line", ring)
    p_ex, p_ey, p_ez, p_hx, p_hy, p_hz, p_r, p_hx2, p_hz2 = (message[i] for i in range(9))
    zero_row = jnp.zeros_like(p_hx)
    hx_prev = shift_down(hx, 1, jnp.where(is_first, zero_row, p_hx))
    hz_prev = shift_down(hz, 1, jnp.where(is_first, zero_row, p_hz))
    ex1 = ex + scaled_rows * (hz - hz_prev)
    ez1 = ez - scaled_rows * (hx - hx_prev)
    hx1 = hx[:, :-1] - COURANT * (ez1[:, 1:] - ez1[:, :-1])
    hz1 = hz[:, :-1] + COURANT * (ex1[:, 1:] - ex1[:, :-1])
    ex_y = p_ex + p_r * (p_hz - p_hz2)
    ez_y = p_ez - p_r * (p_hx - p_hx2)
    ex_next = jnp.where(is_first, zero_row, ex1[:, :1])
    ez_next = jnp.where(is_first, zero_row, ez1[:, :1])
    hx_y = p_hx - COURANT * (ez_next - ez_y)
    hz_y = p_hz + COURANT * (ex_next - ex_y)
    fields = (
        jnp.concatenate([ex_y, ex1[:, :-1]], 1),
        jnp.concatenate([p_ey, ey[:, :-1]], 1),
        jnp.concatenate([ez_y, ez1[:, :-1]], 1),
        jnp.concatenate([hx_y, hx1], 1),
        jnp.concatenate([p_hy, hy[:, :-1]], 1),
        jnp.concatenate([hz_y, hz1], 1),
    )
    scaled_held = jnp.concatenate([p_r[:eps_planes], scaled_rows[:, :-1]], 1)
    inverse_cols = None
    for instant in range(step_count):
        if instant > 0:
            amplitude = jnp.cos(frequency * (instant + 1))
            x_local = offset + jnp.arange(strip, dtype=jnp.int32)
            column_local = (x_local == plane_at).astype(jnp.float32)
            ex, ey, ez, hx, hy, hz = fields
            ez = ez + (amplitude * column_local[None, :, None]) * port_mode[None, None, :]
            fields = curl_y((ex, ey, ez, hx, hy, hz), COURANT * inverse_cols, 2)
            rounded = jnp.stack(fields).reshape(comps, strip, line_cells).astype(jnp.bfloat16)
            solved = solve_turned(turn_rows(rounded, line_count), inverse)
        else:
            rounded = jnp.stack(fields).astype(jnp.bfloat16)
            solved = line_solve(rounded, inverse)
        solved = solved.reshape(6, planes, strip, line_cells)
        fields = curl_xz(
            tuple(solved[i] for i in range(6)), scaled_held if instant == 0 else scaled_rows, 2, 0
        )
        stacked = jnp.stack(fields).reshape(comps, strip, line_cells)
        if inverse_cols is None:
            stacked = jnp.concatenate([stacked] + bf16_parts(inverse_rows), 0)
        turned = turn_rows(stacked.astype(jnp.bfloat16), line_count)
        if inverse_cols is None:
            width = eps_planes * strip
            pieces = [
                turned[:, comps * strip + k * width : comps * strip + (k + 1) * width].astype(jnp.float32)
                for k in range(2)
            ]
            joined = pieces[0] + pieces[1]
            inverse_cols = joined.T.reshape(eps_planes, strip, line_cells)
            turned = turned[:, : comps * strip]
        if instant == 0:
            turned = jnp.roll(turned, -1, axis=0)
        solved = solve_turned(turned, inverse)
        solved = solved.reshape(6, planes, strip, line_cells)
        fields = tuple(solved[i] for i in range(6))
        snapshot = fwd_e[instant].astype(jnp.float32)
        intersection = fields[0] * snapshot[0] + fields[1] * snapshot[1] + fields[2] * snapshot[2]
        gradient = gradient + mask_weight * intersection * (inverse_cols * inverse_cols)
    out = jnp.stack(fields)
    return (out[:3], out[3:], gradient)


def solution(mesh):
    in_specs = (
        P(None, "exc", "line", None),
        P(None, "exc", "line", None),
        P(None, None, "exc", "line", None),
        P(None, "line", None),
        P(None, "line", None),
        P(),
        P("exc"),
        P("exc"),
        P("exc"),
    )
    out_specs = (P(None, "exc", "line", None), P(None, "exc", "line", None), P("exc", "line", None))
    return jax.shard_map(
        per_device, mesh=mesh, in_specs=in_specs, out_specs=out_specs, check_vma=False
    )
```

```python
import jax
import jax.numpy as jnp
from jax import lax
from jax.sharding import PartitionSpec as P

COURANT = 0.4


def line_solve(rounded, inverse):
    flattened = rounded.reshape(-1, rounded.shape[-1])
    solved = lax.dot_general(
        flattened, inverse, (((1,), (1,)), ((), ())), preferred_element_type=jnp.float32
    )
    return solved.reshape(rounded.shape)


def turn_rows(block, line_count):
    comps, strip, cells = block.shape
    parts = block.reshape(comps, strip, line_count, strip)
    parts = jnp.transpose(parts, (2, 1, 0, 3)).reshape(line_count, strip, comps * strip)
    parts = lax.all_to_all(parts, "line", 0, 0, tiled=True)
    return parts.reshape(line_count * strip, comps * strip)


def solve_turned(turned, inverse):
    return lax.dot_general(
        turned, inverse, (((0,), (1,)), ((), ())), preferred_element_type=jnp.float32
    )


def bf16_parts(values):
    high = lax.reduce_precision(values, exponent_bits=8, mantissa_bits=7)
    return [high, values - high]


def shift_down(f, along, first):
    inner = f.shape[along]
    return jnp.concatenate([first, lax.slice_in_dim(f, 0, inner - 1, axis=along)], axis=along)


def shift_up(f, along, last):
    inner = f.shape[along]
    return jnp.concatenate([lax.slice_in_dim(f, 1, inner, axis=along), last], axis=along)


def zeros_like_slice(f, along):
    shape = list(f.shape)
    shape[along] = 1
    return jnp.zeros(shape, f.dtype)


def curl_y(fields, scaled, along, below=None, above=None):
    ex, ey, ez, hx, hy, hz = fields
    if below is None:
        below = (zeros_like_slice(hx, along), zeros_like_slice(hz, along))
    if above is None:
        z = zeros_like_slice(hx, along)
        above = (z, z, z, z, z)
    hx_prev = shift_down(hx, along, below[0])
    hz_prev = shift_down(hz, along, below[1])
    ex = ex + scaled * (hz - hz_prev)
    ez = ez - scaled * (hx - hx_prev)
    last = lax.slice_in_dim(hx, hx.shape[along] - 1, hx.shape[along], axis=along)
    last_z = lax.slice_in_dim(hz, hz.shape[along] - 1, hz.shape[along], axis=along)
    ex_a, ez_a, hx_a, hz_a, scaled_a = above
    ex_next_edge = ex_a + scaled_a * (hz_a - last_z)
    ez_next_edge = ez_a - scaled_a * (hx_a - last)
    ex_next = shift_up(ex, along, ex_next_edge)
    ez_next = shift_up(ez, along, ez_next_edge)
    hx = hx - COURANT * (ez_next - ez)
    hz = hz + COURANT * (ex_next - ex)
    return (ex, ey, ez, hx, hy, hz)


def curl_xz(fields, scaled, along_x, along_z):
    ex, ey, ez, hx, hy, hz = fields

    def lower(f, along):
        return f - shift_down(f, along, zeros_like_slice(f, along))

    def upper(f, along):
        return shift_up(f, along, zeros_like_slice(f, along)) - f

    ex = ex - scaled * lower(hy, along_z)
    ey = ey + scaled * (lower(hx, along_z) - lower(hz, along_x))
    ez = ez + scaled * lower(hy, along_x)
    hx = hx + COURANT * upper(ey, along_z)
    hy = hy + COURANT * (upper(ez, along_x) - upper(ex, along_z))
    hz = hz - COURANT * upper(ey, along_x)
    return (ex, ey, ez, hx, hy, hz)


def per_device(
    adj_e, adj_h, fwd_e, permittivity, design_mask, inverse, omega, port_mode, port_plane
):
    line_cells = inverse.shape[0]
    strip = adj_e.shape[2]
    planes = adj_e.shape[1]
    eps_planes = permittivity.shape[0]
    step_count = fwd_e.shape[0]
    line_count = lax.axis_size("line")
    index = lax.axis_index("line")
    offset = index * strip
    inverse_rows = 1.0 / permittivity
    scaled_rows = COURANT * inverse_rows
    frequency = omega[0]
    plane_at = port_plane[0]
    mask_weight = design_mask.astype(jnp.float32)
    gradient = jnp.zeros(design_mask.shape, jnp.float32)
    comps = 6 * planes

    column = (jnp.arange(line_cells, dtype=jnp.int32) == plane_at).astype(jnp.float32)
    profile_rows = lax.dynamic_slice_in_dim(port_mode, offset, strip)
    amplitude = jnp.cos(frequency * 1.0)
    ex, ey, ez = adj_e[0], adj_e[1], adj_e[2]
    hx, hy, hz = adj_h[0], adj_h[1], adj_h[2]
    ez = ez + (amplitude * profile_rows[None, :, None]) * column[None, None, :]
    is_first = index == 0
    ring = [(i, (i + 1) % line_count) for i in range(line_count)]
    scaled_planes = jnp.broadcast_to(scaled_rows, ex.shape)
    message = jnp.stack(
        [f[:, -1:] for f in (ex, ey, ez, hx, hy, hz, scaled_planes)] + [hx[:, -2:-1], hz[:, -2:-1]]
    )
    message = lax.ppermute(message, "line", ring)
    p_ex, p_ey, p_ez, p_hx, p_hy, p_hz, p_r, p_hx2, p_hz2 = (message[i] for i in range(9))
    zero_row = jnp.zeros_like(p_hx)
    hx_prev = shift_down(hx, 1, jnp.where(is_first, zero_row, p_hx))
    hz_prev = shift_down(hz, 1, jnp.where(is_first, zero_row, p_hz))
    ex1 = ex + scaled_rows * (hz - hz_prev)
    ez1 = ez - scaled_rows * (hx - hx_prev)
    hx1 = hx[:, :-1] - COURANT * (ez1[:, 1:] - ez1[:, :-1])
    hz1 = hz[:, :-1] + COURANT * (ex1[:, 1:] - ex1[:, :-1])
    ex_y = p_ex + p_r * (p_hz - p_hz2)
    ez_y = p_ez - p_r * (p_hx - p_hx2)
    ex_next = jnp.where(is_first, zero_row, ex1[:, :1])
    ez_next = jnp.where(is_first, zero_row, ez1[:, :1])
    hx_y = p_hx - COURANT * (ez_next - ez_y)
    hz_y = p_hz + COURANT * (ex_next - ex_y)
    fields = (
        jnp.concatenate([ex_y, ex1[:, :-1]], 1),
        jnp.concatenate([p_ey, ey[:, :-1]], 1),
        jnp.concatenate([ez_y, ez1[:, :-1]], 1),
        jnp.concatenate([hx_y, hx1], 1),
        jnp.concatenate([p_hy, hy[:, :-1]], 1),
        jnp.concatenate([hz_y, hz1], 1),
    )
    scaled_held = jnp.concatenate([p_r[:eps_planes], scaled_rows[:, :-1]], 1)
    inverse_held = jnp.roll(inverse, 1, axis=1)
    inverse_cols = None
    for instant in range(step_count):
        if instant > 0:
            amplitude = jnp.cos(frequency * (instant + 1))
            x_local = offset + jnp.arange(strip, dtype=jnp.int32)
            column_local = (x_local == plane_at).astype(jnp.float32)
            ex, ey, ez, hx, hy, hz = fields
            ez = ez + (amplitude * column_local[None, :, None]) * port_mode[None, None, :]
            fields = curl_y((ex, ey, ez, hx, hy, hz), COURANT * inverse_cols, 2)
            rounded = jnp.stack(fields).reshape(comps, strip, line_cells).astype(jnp.bfloat16)
            solved = solve_turned(turn_rows(rounded, line_count), inverse)
        else:
            rounded = jnp.stack(fields).astype(jnp.bfloat16)
            solved = line_solve(rounded, inverse)
        solved = solved.reshape(6, planes, strip, line_cells)
        fields = curl_xz(
            tuple(solved[i] for i in range(6)), scaled_held if instant == 0 else scaled_rows, 2, 0
        )
        stacked = jnp.stack(fields).reshape(comps, strip, line_cells)
        if inverse_cols is None:
            stacked = jnp.concatenate([stacked] + bf16_parts(inverse_rows), 0)
        turned = turn_rows(stacked.astype(jnp.bfloat16), line_count)
        if inverse_cols is None:
            width = eps_planes * strip
            pieces = [
                turned[:, comps * strip + k * width : comps * strip + (k + 1) * width].astype(jnp.float32)
                for k in range(2)
            ]
            joined = pieces[0] + pieces[1]
            inverse_cols = joined.T.reshape(eps_planes, strip, line_cells)
            turned = turned[:, : comps * strip]
        held = inverse_held if instant == 0 else inverse
        half = 3 * planes * strip
        solved_e = solve_turned(turned[:, :half], held).reshape(3, planes, strip, line_cells)
        solved_h = solve_turned(turned[:, half:], held).reshape(3, planes, strip, line_cells)
        fields = tuple(solved_e[i] for i in range(3)) + tuple(solved_h[i] for i in range(3))
        snapshot = fwd_e[instant].astype(jnp.float32)
        intersection = fields[0] * snapshot[0] + fields[1] * snapshot[1] + fields[2] * snapshot[2]
        gradient = gradient + mask_weight * intersection * (inverse_cols * inverse_cols)
    return (solved_e, solved_h, gradient)


def solution(mesh):
    in_specs = (
        P(None, "exc", "line", None),
        P(None, "exc", "line", None),
        P(None, None, "exc", "line", None),
        P(None, "line", None),
        P(None, "line", None),
        P(),
        P("exc"),
        P("exc"),
        P("exc"),
    )
    out_specs = (P(None, "exc", "line", None), P(None, "exc", "line", None), P("exc", "line", None))
    return jax.shard_map(
        per_device, mesh=mesh, in_specs=in_specs, out_specs=out_specs, check_vma=False
    )
```
